512 devices in a mesh: wide: 64 (over z_hi, x, y, core), narrow: 8 (over z_lo).
Axes of the slice: x: 4, y: 4, z: 16 (z_hi: 2, z_lo: 8; z = z_hi * 8 + z_lo), core: 2. Of those that a mesh axis runs over, the one named last changes fastest.
Arguments:
- adjoint_start: float32 [2, 20, 1024, 4096], P(None, None, 'wide', 'narrow'), may hold values from -6 to 6
- velocity: float32 [2, 20, 1024, 4096], P(None, None, 'wide', 'narrow'), may hold values from -6 to 6
- coupling: float32 [19, 1024, 4096], P(None, 'wide', 'narrow'), may hold values from 30 to 300
- friction: float32 [1024, 4096], P('wide', 'narrow'), may hold values from 0.1 to 10
- horiz: float32 [1024, 4096], P('wide', 'narrow'), may hold values from 0.1 to 1
- ice_mask: int32 [1024, 4096], P('wide', 'narrow'), may hold values 0 or 1
- obs_owner: int32 [8, 262144, 1], P('narrow', 'wide'), may hold values from 0 to 63; in each aligned block of 4096 rows (0 to 4095, 4096 to 8191, ..., all dimensions but the last counted through in order) at most 128 rows name the same one
- obs_cell: int32 [8, 262144], P('narrow', 'wide'), may hold values from 0 to 8191
- obs_value: float32 [2, 8, 262144], P(None, 'narrow', 'wide'), may hold values from -6 to 6
- obs_weight: float32 [8, 262144], P('narrow', 'wide'), may hold values from 0.1 to 1
Outputs:
- adjoint: float32 [2, 20, 1024, 4096], P(None, None, 'wide', 'narrow')
- direction: float32 [1024, 4096], P('wide', 'narrow')
- misfit: float32 [], replicated
The draws below stay inside these ranges and needn't reach their ends.
Inputs may be any that keep to these rules, and one draw needn't show every extreme that they name: `obs_owner`: among the 4096 observations of one device, at most 128 name the same owner.
All inputs are finite; a program needn't handle non-finite values. No bound on the sum of `ice_mask` on one device may be relied on, other than what follows from the above.
Results may differ from the reference program's by a relative error of at most 0.0003.
Values sent between devices are 32-bit elements; how exact they have to be, the bound alone decides.
No kernel may reach another device: no remote copies, remote signals or barrier semaphores. Data moves between devices by JAX's collectives and lax.ppermute only.
A program may use at most 128 MiB of HBM per device.

```python
import math
import jax
import jax.numpy as jnp
import numpy as np
from jax import lax

L = 20
ITERS = 2
CX = 16
CY = 512
OBS_DEV = 4096
CAP = 128
OBS_ALL = 262144
NX = 1024
NY = 4096
KAPPA = 1024
N_WIDE = 64
N_NARROW = 8


def plant(values, stream_key, smallest, high):
    shape = values.shape
    spot = [jax.random.randint(jax.random.fold_in(stream_key, axis), (), 0, shape[axis]) for axis in range(len(shape))]
    values = values.at[tuple(spot)].set(smallest)
    longest = shape.index(max(shape))
    spot[longest] = (spot[longest] + 1) % shape[longest]
    return values.at[tuple(spot)].set(high)


def block_levels(stream_key, dims, pieces, smallest, top_value):
    def one(dim, blocks):
        steps = jax.random.uniform(jax.random.fold_in(jax.random.fold_in(stream_key, 6), dim), (blocks,), jnp.float32, smallest / len(pieces), top_value / len(pieces))
        return jnp.repeat(jnp.exp(steps), dims[dim] // blocks).reshape((-1,) + (1,) * (len(dims) - dim - 1))

    level = one(*pieces[0])
    for cut in pieces[1:]:
        level = level * one(*cut)
    return level


def assign_block(rng, own, number, rows, number_of, top, most, lean):
    order = jax.random.permutation(rng, number_of)
    heavy_load, usual = shares(number_of, rows * top, most, lean, True), shares(number_of, rows * top, most, lean, False)
    places = jnp.arange(number_of)

    def named(sizes, offset_by):
        used = int((sizes > 0).sum())
        fixed = max(1, used // 4)
        moved = fixed + (places - fixed + offset_by * (used - fixed)) % max(1, number_of - fixed)
        return jnp.zeros((number_of,), jnp.int32).at[order[jnp.where(places < fixed, places, moved)]].set(jnp.asarray(sizes, jnp.int32))

    sizes = jnp.where(number % 4 == 0, named(heavy_load, number // 4), named(usual, number - number // 4 - 1))
    mixed = jax.random.permutation(jax.random.fold_in(own, 3), number_of)
    giver, receiver = mixed[0:number_of // 2 * 2:2], mixed[1:number_of // 2 * 2:2]
    room = jnp.minimum(sizes[giver] - 1, most - sizes[receiver]) // 2
    room = jnp.where((giver == order[0]) | (receiver == order[0]) | (sizes[receiver] == 0), 0, jnp.maximum(room, 0))
    moved = jax.random.randint(jax.random.fold_in(own, 4), (number_of // 2,), 0, 1 << 20) % (room + 1)
    sizes = sizes.at[giver].add(-moved).at[receiver].add(moved)
    members = jnp.searchsorted(jnp.cumsum(sizes), jnp.arange(rows * top), side="right").astype(jnp.int32)
    table = members.reshape(top, rows).T
    table = table[jax.random.permutation(jax.random.fold_in(own, 1), rows)]
    offset_by = jax.random.randint(jax.random.fold_in(own, 2), (rows, 1), 0, top)
    return jnp.take_along_axis(table, (jnp.arange(top)[None, :] + offset_by) % top, axis=1)


def shares(count, total, most, skew, full):
    weights = [(1 << 20) // math.isqrt(grade ** skew) + 1 for grade in range(1, count + 1)]
    largest = most if full else min(most, max(-(-total // count), total * weights[0] // sum(weights)))
    least = 1 if total - largest >= count - 1 else 0
    given, spare = [largest] + [least] * (count - 1), total - largest - least * (count - 1)
    while spare > 0:
        candidates = [i for i in range(1, count) if given[i] < largest] or [i for i in range(1, count) if given[i] < most]
        pool, left = sum([weights[i] for i in candidates]), spare
        for i in candidates:
            addition = min(most - given[i], max(1, left * weights[i] // pool), spare)
            given[i] = given[i] + addition
            spare = spare - addition
    return np.array(given)


def centred(rng, dims, scale, reach, split=(), kind=jnp.bfloat16):
    drawn = jax.random.normal(rng, dims, jnp.float32) * scale
    if len(split) > 0:
        drawn = block_levels(rng, dims, split, -0.22, 0.18) * drawn
    return jnp.clip(drawn, min=-reach, max=reach).astype(kind)


def setup_inputs(seed: int = 0) -> dict:
    keys = jax.random.split(jax.random.key(seed), 11)
    adjoint_start = centred(keys[0], (2, L, NX, NY), 1.0, 6.0, ((2, 64), (3, 8)), jnp.float32)
    velocity = centred(keys[1], (2, L, NX, NY), 1.0, 6.0, ((2, 64), (3, 8)), jnp.float32)
    coupling = jnp.clip(jnp.exp(math.log(300.0) - 2.3025851 * jax.random.uniform(keys[2], (L - 1, NX, NY), jnp.float32) ** block_levels(keys[2], (L - 1, NX, NY), ((1, 64), (2, 8)), -0.2, 0.2)), 30.0, 300.0)
    friction = jnp.clip(jnp.exp(math.log(10.0) - 4.6051702 * jax.random.uniform(keys[3], (NX, NY), jnp.float32) ** block_levels(keys[3], (NX, NY), ((0, 64), (1, 8)), -0.2, 0.2)), 0.1, 10.0)
    horiz = jnp.clip(jnp.exp(math.log(1.0) - 2.3025851 * jax.random.uniform(keys[4], (NX, NY), jnp.float32) ** block_levels(keys[4], (NX, NY), ((0, 64), (1, 8)), -0.2, 0.2)), 0.1, 1.0)
    ice_mask = plant((jax.random.randint(keys[5], (NX, NY), 0, 10) < 9).astype(jnp.int32), jax.random.fold_in(keys[5], 1), 0, 1)
    obs_owner_keys = jax.random.split(jax.random.fold_in(keys[6], 1), N_NARROW * OBS_ALL // OBS_DEV)
    obs_owner_turns = jax.random.permutation(jax.random.fold_in(keys[6], 3), N_NARROW * OBS_ALL // OBS_DEV)
    obs_owner = jax.vmap(lambda own, number: assign_block(jax.random.fold_in(keys[6], 2), own, number, OBS_DEV, N_WIDE, 1, CAP, 2))(obs_owner_keys, obs_owner_turns).reshape((N_NARROW, OBS_ALL, 1))
    obs_cell = plant(jax.random.randint(keys[7], (N_NARROW, OBS_ALL), 0, CX * CY), jax.random.fold_in(keys[7], 1), 0, (CX * CY) - 1).astype(jnp.int32)
    obs_value = centred(keys[8], (2, N_NARROW, OBS_ALL), 1.0, 6.0, ((1, 8), (2, 64)), jnp.float32)
    obs_weight = jnp.clip(jnp.exp(math.log(1.0) - 2.3025851 * jax.random.uniform(keys[9], (N_NARROW, OBS_ALL), jnp.float32) ** block_levels(keys[9], (N_NARROW, OBS_ALL), ((0, 8), (1, 64)), -0.2, 0.2)), 0.1, 1.0)
    return dict(adjoint_start=adjoint_start, velocity=velocity, coupling=coupling, friction=friction, horiz=horiz, ice_mask=ice_mask, obs_owner=obs_owner, obs_cell=obs_cell, obs_value=obs_value, obs_weight=obs_weight)


def thomas(coupling, diagonal, right_side):
    layers = diagonal.shape[0]
    pivots = diagonal[0]
    ratios = [coupling[0] / pivots]
    partial_sol = [right_side[:, 0] / pivots]
    for level in range(1, layers):
        pivots = diagonal[level] - coupling[level - 1] * ratios[level - 1]
        if level < layers - 1:
            ratios.append(coupling[level] / pivots)
        partial_sol.append((right_side[:, level] + coupling[level - 1] * partial_sol[level - 1]) / pivots)
    result = [partial_sol[layers - 1]]
    for level in range(layers - 2, -1, -1):
        result.append(partial_sol[level] + ratios[level] * result[-1])
    ordered = result[::-1]
    return jnp.stack(ordered, axis=1)

def make_diagonal(coupling, friction, horiz):
    zeros_row = jnp.zeros_like(coupling[:1])
    below = jnp.concatenate([zeros_row, coupling], axis=0)
    above = jnp.concatenate([coupling, zeros_row], axis=0)
    diagonal = 0.5 + 4.0 * horiz[None] + below + above
    return diagonal.at[0].add(friction)

def relax(padded, coupling, diagonal, horiz, ice_float, force):
    beside_all = padded[..., 2:, 1:-1] + padded[..., :-2, 1:-1] + padded[..., 1:-1, 2:] + padded[..., 1:-1, :-2]
    right_side = horiz * beside_all
    right_side = right_side.at[:, -1].add(force)
    return ice_float * thomas(coupling, diagonal, right_side)

def smooth_lines(source, kappa_val):
    length = source.shape[0]
    main_band = jnp.full((length,), 1.0 + 2.0 * kappa_val, source.dtype)
    main_band = main_band.at[0].set(1.0 + kappa_val).at[-1].set(1.0 + kappa_val)
    lower_band = jnp.full((length,), -kappa_val, source.dtype).at[0].set(0.0)
    upper_band = jnp.full((length,), -kappa_val, source.dtype).at[-1].set(0.0)
    return lax.linalg.tridiagonal_solve(lower_band, main_band, upper_band, source)

def reference(adjoint_start, velocity, coupling, friction, horiz, ice_mask, obs_owner, obs_cell, obs_value, obs_weight):
    strip_row = jnp.broadcast_to(jnp.arange(N_NARROW, dtype=jnp.int32)[:, None], obs_cell.shape)
    owners = obs_owner[..., 0].astype(jnp.int32)
    row_x = owners * CX + obs_cell // CY
    row_y = strip_row * CY + obs_cell % CY
    flat_ids = (row_x * NY + row_y).reshape(-1).astype(jnp.int32)
    surface = velocity[:, L - 1].reshape(2, NX * NY)[:, flat_ids]
    residual = surface - obs_value.reshape(2, -1)
    weights = obs_weight.reshape(-1)
    force = jnp.zeros((2, NX * NY), velocity.dtype).at[:, flat_ids].add(weights * residual).reshape(2, NX, NY)
    misfit = 0.5 * jnp.sum(weights * lax.optimization_barrier(jnp.sum(residual * residual, axis=0)))
    ice_float = ice_mask.astype(velocity.dtype)
    diagonal = make_diagonal(coupling, friction, horiz)
    adjoint = adjoint_start
    for sweep_no in range(ITERS):
        padded = jnp.pad(adjoint, ((0, 0), (0, 0), (1, 1), (1, 1)))
        adjoint = relax(padded, coupling, diagonal, horiz, ice_float, force)
    grad = -friction * ice_float * lax.optimization_barrier(jnp.sum(adjoint[:, 0] * velocity[:, 0], axis=0))
    smooth = smooth_lines(grad, float(KAPPA))
    mean_square = jnp.sum(smooth * smooth) / (NX * NY)
    direction = smooth * lax.rsqrt(mean_square + 1e-06)
    return (adjoint, direction, misfit)
```

```python
import jax
import jax.numpy as jnp
from jax import lax
from jax.sharding import PartitionSpec as P

ITERS = 2
KAPPA = 1024


def padded_2(value, sides, width):
    for axis, dim in sides:
        peers, length = (lax.axis_size(axis), value.shape[dim])
        up = [(i, (i + 1) % peers) for i in range(peers - 1)]
        down = [(j, i) for i, j in up]
        last = lax.slice_in_dim(value, length - width, length, axis=dim)
        first = lax.slice_in_dim(value, 0, width, axis=dim)
        before = lax.ppermute(last, axis, up)
        after = lax.ppermute(first, axis, down)
        value = jnp.concatenate([before, value, after], axis=dim)
    return value


def thomas(coupling, diagonal, right_side):
    layers = diagonal.shape[0]
    pivots = diagonal[0]
    ratios = [coupling[0] / pivots]
    partial_sol = [right_side[:, 0] / pivots]
    for level in range(1, layers):
        pivots = diagonal[level] - coupling[level - 1] * ratios[level - 1]
        if level < layers - 1:
            ratios.append(coupling[level] / pivots)
        partial_sol.append(
            (right_side[:, level] + coupling[level - 1] * partial_sol[level - 1]) / pivots
        )
    result = [partial_sol[layers - 1]]
    for level in range(layers - 2, -1, -1):
        result.append(partial_sol[level] + ratios[level] * result[-1])
    ordered = result[::-1]
    return jnp.stack(ordered, axis=1)


def make_diagonal(coupling, friction, horiz):
    zeros_row = jnp.zeros_like(coupling[:1])
    below = jnp.concatenate([zeros_row, coupling], axis=0)
    above = jnp.concatenate([coupling, zeros_row], axis=0)
    diagonal = 0.5 + 4.0 * horiz[None] + below + above
    return diagonal.at[0].add(friction)


def relax(padded, coupling, diagonal, horiz, ice_float, force):
    beside_all = (
        padded[..., 2:, 1:-1]
        + padded[..., :-2, 1:-1]
        + padded[..., 1:-1, 2:]
        + padded[..., 1:-1, :-2]
    )
    right_side = horiz * beside_all
    right_side = right_side.at[:, -1].add(force)
    return ice_float * thomas(coupling, diagonal, right_side)


def smooth_lines(source, kappa_val):
    length = source.shape[0]
    cell_index = lax.broadcasted_iota(jnp.int32, (length, length), 0)
    freq_index = lax.broadcasted_iota(jnp.int32, (length, length), 1)
    wave_phase = freq_index * (2 * cell_index + 1) % (4 * length)
    norm_factor = jnp.where(freq_index == 0, jnp.sqrt(1.0 / length), jnp.sqrt(2.0 / length)).astype(
        jnp.float32
    )
    cosine_table = jnp.cos(jnp.pi * wave_phase.astype(jnp.float32) / (2.0 * length)) * norm_factor
    modes = lax.iota(jnp.int32, length).astype(jnp.float32)
    spectrum = 1.0 + kappa_val * (2.0 - 2.0 * jnp.cos(jnp.pi * modes / length))
    coefficients = lax.dot_general(
        cosine_table,
        source,
        (((0,), (0,)), ((), ())),
        precision=lax.Precision.HIGHEST,
        preferred_element_type=jnp.float32,
    )
    coefficients = coefficients / spectrum[:, None]
    return jnp.dot(
        cosine_table,
        coefficients,
        precision=lax.Precision.HIGHEST,
        preferred_element_type=jnp.float32,
    )


def split_parts(value):
    high = lax.reduce_precision(value, exponent_bits=8, mantissa_bits=7)
    rest = value - high
    middle = lax.reduce_precision(rest, exponent_bits=8, mantissa_bits=7)
    low = rest - middle
    return jnp.concatenate([high, middle, low], axis=0).astype(jnp.bfloat16)


def exact_dot(value, selector, contract):
    rows = value.shape[0]
    parts = lax.dot_general(
        split_parts(value),
        selector,
        (((1,), (contract,)), ((), ())),
        preferred_element_type=jnp.float32,
    )
    parts = parts.reshape(3, rows, parts.shape[-1])
    return (parts[0] + parts[1]) + parts[2]


def owner_ranks(owner_hot):
    count, peers = owner_hot.shape
    block = 128
    blocks = count // block
    hot = owner_hot.astype(jnp.bfloat16).reshape(blocks, block, peers)
    lower = (
        lax.broadcasted_iota(jnp.int32, (block, block), 0)
        >= lax.broadcasted_iota(jnp.int32, (block, block), 1)
    ).astype(jnp.bfloat16)
    within = jnp.einsum("ij,bjw->biw", lower, hot, preferred_element_type=jnp.float32)
    totals = within[:, -1, :].astype(jnp.bfloat16)
    strict = (
        lax.broadcasted_iota(jnp.int32, (blocks, blocks), 0)
        > lax.broadcasted_iota(jnp.int32, (blocks, blocks), 1)
    ).astype(jnp.bfloat16)
    before = jnp.dot(strict, totals, preferred_element_type=jnp.float32)
    counts = within + before[:, None, :]
    mine = jnp.where(owner_hot.reshape(blocks, block, peers), counts, 0.0)
    return jnp.sum(mine, axis=-1).reshape(count) - 1.0


def on_device(
    adjoint_start,
    velocity,
    coupling,
    friction,
    horiz,
    ice_mask,
    obs_owner,
    obs_cell,
    obs_value,
    obs_weight,
):
    wide_count = lax.axis_size("wide")
    rows_x, rows_y = friction.shape
    owners = obs_owner[0, :, 0]
    cell_ids = obs_cell[0]
    how_many = owners.shape[0]
    capacity = 2 * how_many // wide_count
    owner_hot = owners[:, None] == jnp.arange(wide_count, dtype=jnp.int32)[None, :]
    ranking = owner_ranks(owner_hot)
    rank_hot = (
        ranking[:, None] == jnp.arange(capacity, dtype=jnp.float32)[None, :]
    ).astype(jnp.bfloat16)
    payload = jnp.stack(
        [obs_value[0, 0], obs_value[1, 0], obs_weight[0], cell_ids.astype(jnp.float32)], axis=0
    )
    spread = jnp.where(owner_hot.T[None, :, :], payload[:, None, :], 0.0)
    packed = exact_dot(spread.reshape(4 * wide_count, how_many), rank_hot, 0)
    packed = packed.reshape(4, wide_count, capacity)
    arrived = lax.all_to_all(packed, "wide", split_axis=1, concat_axis=1, tiled=True).reshape(4, -1)
    target = arrived[3].astype(jnp.int32)
    slots = target.shape[0]
    column_hot = (
        jnp.arange(rows_y, dtype=jnp.int32)[:, None] == (target % rows_y)[None, :]
    ).astype(jnp.bfloat16)
    row_hot = jnp.arange(rows_x, dtype=jnp.int32)[:, None] == (target // rows_y)[None, :]
    top = velocity[:, -1].reshape(2 * rows_x, rows_y)
    picked = exact_dot(top, column_hot, 0).reshape(2, rows_x, slots)
    surface = jnp.sum(jnp.where(row_hot[None], picked, 0.0), axis=1)
    residual = surface - arrived[:2]
    weights = arrived[2]
    weighted = weights * residual
    placed = jnp.where(row_hot[None], weighted[:, None, :], 0.0).reshape(2 * rows_x, slots)
    force = exact_dot(placed, column_hot, 1).reshape(2, rows_x, rows_y)
    local_misfit = 0.5 * jnp.sum(weights * jnp.sum(residual * residual, axis=0))
    ice_float = ice_mask.astype(jnp.float32)
    diagonal = make_diagonal(coupling, friction, horiz)
    adjoint = adjoint_start
    for sweep_no in range(ITERS):
        padded = padded_2(adjoint, (("wide", 2), ("narrow", 3)), 1)
        adjoint = relax(padded, coupling, diagonal, horiz, ice_float, force)
    grad = -friction * ice_float * jnp.sum(adjoint[:, 0] * velocity[:, 0], axis=0)
    sent = jnp.concatenate([grad, jnp.broadcast_to(local_misfit, (1, rows_y))], axis=0)
    slab = lax.all_to_all(sent, "wide", split_axis=1, concat_axis=0, tiled=True)
    slab = slab.reshape(wide_count, rows_x + 1, -1)
    wide_misfit = jnp.sum(slab[:, rows_x, 0])
    slab = slab[:, :rows_x].reshape(wide_count * rows_x, -1)
    smooth = smooth_lines(slab, float(KAPPA))
    local_square = jnp.sum(smooth * smooth)
    lines = smooth.reshape(wide_count, rows_x, -1)
    square_row = jnp.broadcast_to(local_square, (wide_count, 1, lines.shape[-1]))
    lines = jnp.concatenate([lines, square_row], axis=1).reshape(wide_count * (rows_x + 1), -1)
    back = lax.all_to_all(lines, "wide", split_axis=0, concat_axis=1, tiled=True)
    wide_square = jnp.sum(back[rows_x].reshape(wide_count, -1)[:, 0])
    back = back[:rows_x]
    totals = lax.psum(jnp.stack([wide_square, wide_misfit]), "narrow")
    cell_total = slab.shape[0] * rows_y * lax.axis_size("narrow")
    direction = back * lax.rsqrt(totals[0] / cell_total + 1e-06)
    return (adjoint, direction, totals[1])


def solution(mesh):
    in_specs = (
        P(None, None, "wide", "narrow"),
        P(None, None, "wide", "narrow"),
        P(None, "wide", "narrow"),
        P("wide", "narrow"),
        P("wide", "narrow"),
        P("wide", "narrow"),
        P("narrow", "wide", None),
        P("narrow", "wide"),
        P(None, "narrow", "wide"),
        P("narrow", "wide"),
    )
    out_specs = (P(None, None, "wide", "narrow"), P("wide", "narrow"), P())
    return jax.shard_map(
        on_device, mesh=mesh, in_specs=in_specs, out_specs=out_specs, check_vma=False
    )
```

```python
import jax
import jax.numpy as jnp
from jax import lax
from jax.sharding import PartitionSpec as P

ITERS = 2
KAPPA = 1024


def neighbour_sum(value):
    edges = []
    for axis, dim in (("wide", 2), ("narrow", 3)):
        peers, length = (lax.axis_size(axis), value.shape[dim])
        up = [(i, i + 1) for i in range(peers - 1)]
        down = [(j, i) for i, j in up]
        last = lax.slice_in_dim(value, length - 1, length, axis=dim)
        first = lax.slice_in_dim(value, 0, 1, axis=dim)
        before = lax.ppermute(last, axis, up)
        after = lax.ppermute(first, axis, down)
        inner_next = lax.slice_in_dim(value, 1, length, axis=dim)
        inner_prev = lax.slice_in_dim(value, 0, length - 1, axis=dim)
        edges.append(jnp.concatenate([inner_next, after], axis=dim))
        edges.append(jnp.concatenate([before, inner_prev], axis=dim))
    return edges[0] + edges[1] + edges[2] + edges[3]


def thomas(coupling, diagonal, right_side):
    layers = diagonal.shape[0]
    pivots = diagonal[0]
    ratios = [coupling[0] / pivots]
    partial_sol = [right_side[:, 0] / pivots]
    for level in range(1, layers):
        pivots = diagonal[level] - coupling[level - 1] * ratios[level - 1]
        if level < layers - 1:
            ratios.append(coupling[level] / pivots)
        partial_sol.append(
            (right_side[:, level] + coupling[level - 1] * partial_sol[level - 1]) / pivots
        )
    result = [partial_sol[layers - 1]]
    for level in range(layers - 2, -1, -1):
        result.append(partial_sol[level] + ratios[level] * result[-1])
    ordered = result[::-1]
    return jnp.stack(ordered, axis=1)


def make_diagonal(coupling, friction, horiz):
    zeros_row = jnp.zeros_like(coupling[:1])
    below = jnp.concatenate([zeros_row, coupling], axis=0)
    above = jnp.concatenate([coupling, zeros_row], axis=0)
    diagonal = 0.5 + 4.0 * horiz[None] + below + above
    return diagonal.at[0].add(friction)


def relax(beside_all, coupling, diagonal, horiz, ice_float, force):
    right_side = horiz * beside_all
    right_side = right_side.at[:, -1].add(force)
    return ice_float * thomas(coupling, diagonal, right_side)


def cosine_table(length):
    block = 32
    freq = lax.broadcasted_iota(jnp.int32, (1, length), 1)
    coarse = lax.broadcasted_iota(jnp.int32, (length // block, 1), 0)
    fine = lax.broadcasted_iota(jnp.int32, (block, 1), 0)
    period = 4 * length
    scale = jnp.pi / (2.0 * length)
    coarse_angle = ((2 * block * coarse * freq) % period).astype(jnp.float32) * scale
    fine_angle = (((2 * fine + 1) * freq) % period).astype(jnp.float32) * scale
    table = (
        jnp.cos(coarse_angle)[:, None, :] * jnp.cos(fine_angle)[None, :, :]
        - jnp.sin(coarse_angle)[:, None, :] * jnp.sin(fine_angle)[None, :, :]
    ).reshape(length, length)
    norm_factor = jnp.where(freq == 0, jnp.sqrt(1.0 / length), jnp.sqrt(2.0 / length))
    return table * norm_factor.astype(jnp.float32)


def smooth_lines(lines, kappa_val):
    length = lines.shape[1]
    table = cosine_table(length)
    modes = lax.iota(jnp.int32, length).astype(jnp.float32)
    spectrum = 1.0 + kappa_val * (2.0 - 2.0 * jnp.cos(jnp.pi * modes / length))
    coefficients = jnp.dot(
        lines, table, precision=lax.Precision.HIGHEST, preferred_element_type=jnp.float32
    )
    coefficients = coefficients / spectrum[None, :]
    return lax.dot_general(
        coefficients,
        table,
        (((1,), (1,)), ((), ())),
        precision=lax.Precision.HIGHEST,
        preferred_element_type=jnp.float32,
    )


def split_parts(value):
    high = lax.reduce_precision(value, exponent_bits=8, mantissa_bits=7)
    rest = value - high
    middle = lax.reduce_precision(rest, exponent_bits=8, mantissa_bits=7)
    low = rest - middle
    return jnp.concatenate([high, middle, low], axis=0).astype(jnp.bfloat16)


def exact_dot(value, selector, contract):
    rows = value.shape[0]
    parts = lax.dot_general(
        split_parts(value),
        selector,
        (((1,), (contract,)), ((), ())),
        preferred_element_type=jnp.float32,
    )
    parts = parts.reshape(3, rows, parts.shape[-1])
    return (parts[0] + parts[1]) + parts[2]


def owner_ranks(owner_hot):
    count, peers = owner_hot.shape
    block = 128
    blocks = count // block
    hot = owner_hot.astype(jnp.bfloat16).reshape(blocks, block, peers)
    lower = (
        lax.broadcasted_iota(jnp.int32, (block, block), 0)
        >= lax.broadcasted_iota(jnp.int32, (block, block), 1)
    ).astype(jnp.bfloat16)
    within = jnp.einsum("ij,bjw->biw", lower, hot, preferred_element_type=jnp.float32)
    totals = within[:, -1, :].astype(jnp.bfloat16)
    strict = (
        lax.broadcasted_iota(jnp.int32, (blocks, blocks), 0)
        > lax.broadcasted_iota(jnp.int32, (blocks, blocks), 1)
    ).astype(jnp.bfloat16)
    before = jnp.dot(strict, totals, preferred_element_type=jnp.float32)
    counts = within + before[:, None, :]
    mine = jnp.where(owner_hot.reshape(blocks, block, peers), counts, 0.0)
    return jnp.sum(mine, axis=-1).reshape(count) - 1.0


def on_device(
    adjoint_start,
    velocity,
    coupling,
    friction,
    horiz,
    ice_mask,
    obs_owner,
    obs_cell,
    obs_value,
    obs_weight,
):
    wide_count = lax.axis_size("wide")
    rows_x, rows_y = friction.shape
    owners = obs_owner[0, :, 0]
    cell_ids = obs_cell[0]
    how_many = owners.shape[0]
    capacity = 2 * how_many // wide_count
    owner_hot = owners[:, None] == jnp.arange(wide_count, dtype=jnp.int32)[None, :]
    ranking = owner_ranks(owner_hot)
    rank_hot = (
        ranking[:, None] == jnp.arange(capacity, dtype=jnp.float32)[None, :]
    ).astype(jnp.bfloat16)
    payload = jnp.stack(
        [obs_value[0, 0], obs_value[1, 0], obs_weight[0], cell_ids.astype(jnp.float32)], axis=0
    )
    spread = jnp.where(owner_hot.T[None, :, :], payload[:, None, :], 0.0)
    packed = exact_dot(spread.reshape(4 * wide_count, how_many), rank_hot, 0)
    packed = packed.reshape(4, wide_count, capacity)
    arrived = lax.all_to_all(packed, "wide", split_axis=1, concat_axis=1, tiled=True).reshape(4, -1)
    target = arrived[3].astype(jnp.int32)
    slots = target.shape[0]
    column_hot = (
        jnp.arange(rows_y, dtype=jnp.int32)[:, None] == (target % rows_y)[None, :]
    ).astype(jnp.bfloat16)
    row_hot = jnp.arange(rows_x, dtype=jnp.int32)[:, None] == (target // rows_y)[None, :]
    top = velocity[:, -1].reshape(2 * rows_x, rows_y)
    picked = exact_dot(top, column_hot, 0).reshape(2, rows_x, slots)
    surface = jnp.sum(jnp.where(row_hot[None], picked, 0.0), axis=1)
    residual = surface - arrived[:2]
    weights = arrived[2]
    weighted = weights * residual
    placed = jnp.where(row_hot[None], weighted[:, None, :], 0.0).reshape(2 * rows_x, slots)
    force = exact_dot(placed, column_hot, 1).reshape(2, rows_x, rows_y)
    local_misfit = 0.5 * jnp.sum(weights * jnp.sum(residual * residual, axis=0))
    ice_float = ice_mask.astype(jnp.float32)
    diagonal = make_diagonal(coupling, friction, horiz)
    adjoint = adjoint_start
    for sweep_no in range(ITERS):
        adjoint = relax(neighbour_sum(adjoint), coupling, diagonal, horiz, ice_float, force)
    grad = -friction * ice_float * jnp.sum(adjoint[:, 0] * velocity[:, 0], axis=0)
    misfit_column = jnp.broadcast_to(local_misfit, (rows_y, 1))
    sent = jnp.concatenate([grad.T, misfit_column], axis=1)
    lines = lax.all_to_all(sent, "wide", split_axis=0, concat_axis=1, tiled=True)
    width = lines.shape[0]
    lines = lines.reshape(width, wide_count, rows_x + 1)
    wide_misfit = jnp.sum(lines[0, :, rows_x])
    lines = lines[:, :, :rows_x].reshape(width, wide_count * rows_x)
    smooth = smooth_lines(lines, float(KAPPA))
    local_square = jnp.sum(smooth * smooth)
    square_column = jnp.broadcast_to(local_square, (width, wide_count, 1))
    returned = jnp.concatenate([smooth.reshape(width, wide_count, rows_x), square_column], axis=2)
    returned = returned.reshape(width, wide_count * (rows_x + 1))
    back = lax.all_to_all(returned, "wide", split_axis=1, concat_axis=0, tiled=True)
    wide_square = jnp.sum(back[::width, rows_x])
    back = back[:, :rows_x].T
    totals = lax.psum(jnp.stack([wide_square, wide_misfit]), "narrow")
    cell_total = wide_count * rows_x * rows_y * lax.axis_size("narrow")
    direction = back * lax.rsqrt(totals[0] / cell_total + 1e-06)
    return (adjoint, direction, totals[1])


def solution(mesh):
    in_specs = (
        P(None, None, "wide", "narrow"),
        P(None, None, "wide", "narrow"),
        P(None, "wide", "narrow"),
        P("wide", "narrow"),
        P("wide", "narrow"),
        P("wide", "narrow"),
        P("narrow", "wide", None),
        P("narrow", "wide"),
        P(None, "narrow", "wide"),
        P("narrow", "wide"),
    )
    out_specs = (P(None, None, "wide", "narrow"), P("wide", "narrow"), P())
    return jax.shard_map(
        on_device, mesh=mesh, in_specs=in_specs, out_specs=out_specs, check_vma=False
    )
```

```python
import jax
import jax.numpy as jnp
from jax import lax
from jax.experimental import pallas as pl
from jax.experimental.pallas import tpu as pltpu
from jax.sharding import PartitionSpec as P

ITERS = 2
KAPPA = 1024


def neighbour_sum(value):
    edges = []
    for axis, dim in (("wide", 2), ("narrow", 3)):
        peers, length = (lax.axis_size(axis), value.shape[dim])
        up = [(i, i + 1) for i in range(peers - 1)]
        down = [(j, i) for i, j in up]
        last = lax.slice_in_dim(value, length - 1, length, axis=dim)
        first = lax.slice_in_dim(value, 0, 1, axis=dim)
        before = lax.ppermute(last, axis, up)
        after = lax.ppermute(first, axis, down)
        inner_next = lax.slice_in_dim(value, 1, length, axis=dim)
        inner_prev = lax.slice_in_dim(value, 0, length - 1, axis=dim)
        edges.append(jnp.concatenate([inner_next, after], axis=dim))
        edges.append(jnp.concatenate([before, inner_prev], axis=dim))
    return edges[0] + edges[1] + edges[2] + edges[3]


def thomas(coupling, diagonal, right_side):
    layers = diagonal.shape[0]
    pivots = diagonal[0]
    ratios = [coupling[0] / pivots]
    partial_sol = [right_side[:, 0] / pivots]
    for level in range(1, layers):
        pivots = diagonal[level] - coupling[level - 1] * ratios[level - 1]
        if level < layers - 1:
            ratios.append(coupling[level] / pivots)
        partial_sol.append(
            (right_side[:, level] + coupling[level - 1] * partial_sol[level - 1]) / pivots
        )
    result = [partial_sol[layers - 1]]
    for level in range(layers - 2, -1, -1):
        result.append(partial_sol[level] + ratios[level] * result[-1])
    ordered = result[::-1]
    return jnp.stack(ordered, axis=1)


def make_diagonal(coupling, friction, horiz):
    zeros_row = jnp.zeros_like(coupling[:1])
    below = jnp.concatenate([zeros_row, coupling], axis=0)
    above = jnp.concatenate([coupling, zeros_row], axis=0)
    diagonal = 0.5 + 4.0 * horiz[None] + below + above
    return diagonal.at[0].add(friction)


def relax(beside_all, coupling, diagonal, horiz, ice_float, force):
    right_side = horiz * beside_all
    right_side = right_side.at[:, -1].add(force)
    return ice_float * thomas(coupling, diagonal, right_side)


def column_kernel(beside_ref, coupling_ref, friction_ref, horiz_ref, ice_ref, force_ref, out_ref, ratio_ref, partial_ref):
    comps, layers = beside_ref.shape[0], beside_ref.shape[1]
    horiz = horiz_ref[...]
    base = 0.5 + 4.0 * horiz

    def diagonal(level):
        value = base
        if level > 0:
            value = value + coupling_ref[level - 1]
        if level < layers - 1:
            value = value + coupling_ref[level]
        if level == 0:
            value = value + friction_ref[...]
        return value

    def right_side(comp, level):
        value = horiz * beside_ref[comp, level]
        if level == layers - 1:
            value = value + force_ref[comp]
        return value

    pivots = diagonal(0)
    ratio_ref[0] = coupling_ref[0] / pivots
    for comp in range(comps):
        partial_ref[comp, 0] = right_side(comp, 0) / pivots
    for level in range(1, layers):
        below = coupling_ref[level - 1]
        pivots = diagonal(level) - below * ratio_ref[level - 1]
        if level < layers - 1:
            ratio_ref[level] = coupling_ref[level] / pivots
        for comp in range(comps):
            partial_ref[comp, level] = (
                right_side(comp, level) + below * partial_ref[comp, level - 1]
            ) / pivots
    ice = ice_ref[...]
    for comp in range(comps):
        result = partial_ref[comp, layers - 1]
        out_ref[comp, layers - 1] = ice * result
        for level in range(layers - 2, -1, -1):
            result = partial_ref[comp, level] + ratio_ref[level] * result
            out_ref[comp, level] = ice * result


def column_solve(beside, coupling, friction, horiz, ice_float, force):
    comps, layers, rows_x, rows_y = beside.shape
    cells = rows_x * rows_y
    return pl.pallas_call(
        column_kernel,
        out_shape=jax.ShapeDtypeStruct(beside.shape, jnp.float32),
        scratch_shapes=[
            pltpu.VMEM((layers - 1, rows_x, rows_y), jnp.float32),
            pltpu.VMEM(beside.shape, jnp.float32),
        ],
        cost_estimate=pl.CostEstimate(
            flops=12 * comps * layers * cells,
            transcendentals=0,
            bytes_accessed=4 * cells * (2 * comps * layers + layers + 4),
        ),
    )(beside, coupling, friction, horiz, ice_float, force)


def cosine_table(length):
    block = 32
    freq = lax.broadcasted_iota(jnp.int32, (1, length), 1)
    coarse = lax.broadcasted_iota(jnp.int32, (length // block, 1), 0)
    fine = lax.broadcasted_iota(jnp.int32, (block, 1), 0)
    period = 4 * length
    scale = jnp.pi / (2.0 * length)
    coarse_angle = ((2 * block * coarse * freq) % period).astype(jnp.float32) * scale
    fine_angle = (((2 * fine + 1) * freq) % period).astype(jnp.float32) * scale
    table = (
        jnp.cos(coarse_angle)[:, None, :] * jnp.cos(fine_angle)[None, :, :]
        - jnp.sin(coarse_angle)[:, None, :] * jnp.sin(fine_angle)[None, :, :]
    ).reshape(length, length)
    norm_factor = jnp.where(freq == 0, jnp.sqrt(1.0 / length), jnp.sqrt(2.0 / length))
    return table * norm_factor.astype(jnp.float32)


def smooth_lines(lines, kappa_val):
    length = lines.shape[1]
    table = cosine_table(length)
    modes = lax.iota(jnp.int32, length).astype(jnp.float32)
    spectrum = 1.0 + kappa_val * (2.0 - 2.0 * jnp.cos(jnp.pi * modes / length))
    coefficients = jnp.dot(
        lines, table, precision=lax.Precision.HIGHEST, preferred_element_type=jnp.float32
    )
    coefficients = coefficients / spectrum[None, :]
    return lax.dot_general(
        coefficients,
        table,
        (((1,), (1,)), ((), ())),
        precision=lax.Precision.HIGHEST,
        preferred_element_type=jnp.float32,
    )


def split_parts(value):
    high = lax.reduce_precision(value, exponent_bits=8, mantissa_bits=7)
    rest = value - high
    middle = lax.reduce_precision(rest, exponent_bits=8, mantissa_bits=7)
    low = rest - middle
    return jnp.concatenate([high, middle, low], axis=0).astype(jnp.bfloat16)


def exact_dot(value, selector, contract):
    rows = value.shape[0]
    parts = lax.dot_general(
        split_parts(value),
        selector,
        (((1,), (contract,)), ((), ())),
        preferred_element_type=jnp.float32,
    )
    parts = parts.reshape(3, rows, parts.shape[-1])
    return (parts[0] + parts[1]) + parts[2]


def owner_ranks(owner_hot):
    count, peers = owner_hot.shape
    block = 128
    blocks = count // block
    hot = owner_hot.astype(jnp.bfloat16).reshape(blocks, block, peers)
    lower = (
        lax.broadcasted_iota(jnp.int32, (block, block), 0)
        >= lax.broadcasted_iota(jnp.int32, (block, block), 1)
    ).astype(jnp.bfloat16)
    within = jnp.einsum("ij,bjw->biw", lower, hot, preferred_element_type=jnp.float32)
    totals = within[:, -1, :].astype(jnp.bfloat16)
    strict = (
        lax.broadcasted_iota(jnp.int32, (blocks, blocks), 0)
        > lax.broadcasted_iota(jnp.int32, (blocks, blocks), 1)
    ).astype(jnp.bfloat16)
    before = jnp.dot(strict, totals, preferred_element_type=jnp.float32)
    counts = within + before[:, None, :]
    mine = jnp.where(owner_hot.reshape(blocks, block, peers), counts, 0.0)
    return jnp.sum(mine, axis=-1).reshape(count) - 1.0


def on_device(
    adjoint_start,
    velocity,
    coupling,
    friction,
    horiz,
    ice_mask,
    obs_owner,
    obs_cell,
    obs_value,
    obs_weight,
):
    wide_count = lax.axis_size("wide")
    rows_x, rows_y = friction.shape
    owners = obs_owner[0, :, 0]
    cell_ids = obs_cell[0]
    how_many = owners.shape[0]
    capacity = 2 * how_many // wide_count
    owner_hot = owners[:, None] == jnp.arange(wide_count, dtype=jnp.int32)[None, :]
    ranking = owner_ranks(owner_hot)
    rank_hot = (
        ranking[:, None] == jnp.arange(capacity, dtype=jnp.float32)[None, :]
    ).astype(jnp.bfloat16)
    payload = jnp.stack(
        [obs_value[0, 0], obs_value[1, 0], obs_weight[0], cell_ids.astype(jnp.float32)], axis=0
    )
    spread = jnp.where(owner_hot.T[None, :, :], payload[:, None, :], 0.0)
    packed = exact_dot(spread.reshape(4 * wide_count, how_many), rank_hot, 0)
    packed = packed.reshape(4, wide_count, capacity)
    arrived = lax.all_to_all(packed, "wide", split_axis=1, concat_axis=1, tiled=True).reshape(4, -1)
    target = arrived[3].astype(jnp.int32)
    slots = target.shape[0]
    column_hot = (
        jnp.arange(rows_y, dtype=jnp.int32)[:, None] == (target % rows_y)[None, :]
    ).astype(jnp.bfloat16)
    row_hot = jnp.arange(rows_x, dtype=jnp.int32)[:, None] == (target // rows_y)[None, :]
    top = velocity[:, -1].reshape(2 * rows_x, rows_y)
    picked = exact_dot(top, column_hot, 0).reshape(2, rows_x, slots)
    surface = jnp.sum(jnp.where(row_hot[None], picked, 0.0), axis=1)
    residual = surface - arrived[:2]
    weights = arrived[2]
    weighted = weights * residual
    placed = jnp.where(row_hot[None], weighted[:, None, :], 0.0).reshape(2 * rows_x, slots)
    force = exact_dot(placed, column_hot, 1).reshape(2, rows_x, rows_y)
    local_misfit = 0.5 * jnp.sum(weights * jnp.sum(residual * residual, axis=0))
    ice_float = ice_mask.astype(jnp.float32)
    adjoint = adjoint_start
    for sweep_no in range(ITERS):
        adjoint = column_solve(neighbour_sum(adjoint), coupling, friction, horiz, ice_float, force)
    grad = -friction * ice_float * jnp.sum(adjoint[:, 0] * velocity[:, 0], axis=0)
    misfit_column = jnp.broadcast_to(local_misfit, (rows_y, 1))
    sent = jnp.concatenate([grad.T, misfit_column], axis=1)
    lines = lax.all_to_all(sent, "wide", split_axis=0, concat_axis=1, tiled=True)
    width = lines.shape[0]
    lines = lines.reshape(width, wide_count, rows_x + 1)
    wide_misfit = jnp.sum(lines[0, :, rows_x])
    lines = lines[:, :, :rows_x].reshape(width, wide_count * rows_x)
    smooth = smooth_lines(lines, float(KAPPA))
    local_square = jnp.sum(smooth * smooth)
    square_column = jnp.broadcast_to(local_square, (width, wide_count, 1))
    returned = jnp.concatenate([smooth.reshape(width, wide_count, rows_x), square_column], axis=2)
    returned = returned.reshape(width, wide_count * (rows_x + 1))
    back = lax.all_to_all(returned, "wide", split_axis=1, concat_axis=0, tiled=True)
    wide_square = jnp.sum(back[::width, rows_x])
    back = back[:, :rows_x].T
    totals = lax.psum(jnp.stack([wide_square, wide_misfit]), "narrow")
    cell_total = wide_count * rows_x * rows_y * lax.axis_size("narrow")
    direction = back * lax.rsqrt(totals[0] / cell_total + 1e-06)
    return (adjoint, direction, totals[1])


def solution(mesh):
    in_specs = (
        P(None, None, "wide", "narrow"),
        P(None, None, "wide", "narrow"),
        P(None, "wide", "narrow"),
        P("wide", "narrow"),
        P("wide", "narrow"),
        P("wide", "narrow"),
        P("narrow", "wide", None),
        P("narrow", "wide"),
        P(None, "narrow", "wide"),
        P("narrow", "wide"),
    )
    out_specs = (P(None, None, "wide", "narrow"), P("wide", "narrow"), P())
    return jax.shard_map(
        on_device, mesh=mesh, in_specs=in_specs, out_specs=out_specs, check_vma=False
    )
```

```python
import jax
import jax.numpy as jnp
from jax import lax
from jax.experimental import pallas as pl
from jax.experimental.pallas import tpu as pltpu
from jax.sharding import PartitionSpec as P

ITERS = 2
KAPPA = 1024


def neighbour_sum(value):
    edges = []
    for axis, dim in (("wide", 2), ("narrow", 3)):
        peers, length = (lax.axis_size(axis), value.shape[dim])
        up = [(i, i + 1) for i in range(peers - 1)]
        down = [(j, i) for i, j in up]
        last = lax.slice_in_dim(value, length - 1, length, axis=dim)
        first = lax.slice_in_dim(value, 0, 1, axis=dim)
        before = lax.ppermute(last, axis, up)
        after = lax.ppermute(first, axis, down)
        inner_next = lax.slice_in_dim(value, 1, length, axis=dim)
        inner_prev = lax.slice_in_dim(value, 0, length - 1, axis=dim)
        edges.append(jnp.concatenate([inner_next, after], axis=dim))
        edges.append(jnp.concatenate([before, inner_prev], axis=dim))
    return edges[0] + edges[1] + edges[2] + edges[3]


def thomas(coupling, diagonal, right_side):
    layers = diagonal.shape[0]
    pivots = diagonal[0]
    ratios = [coupling[0] / pivots]
    partial_sol = [right_side[:, 0] / pivots]
    for level in range(1, layers):
        pivots = diagonal[level] - coupling[level - 1] * ratios[level - 1]
        if level < layers - 1:
            ratios.append(coupling[level] / pivots)
        partial_sol.append(
            (right_side[:, level] + coupling[level - 1] * partial_sol[level - 1]) / pivots
        )
    result = [partial_sol[layers - 1]]
    for level in range(layers - 2, -1, -1):
        result.append(partial_sol[level] + ratios[level] * result[-1])
    ordered = result[::-1]
    return jnp.stack(ordered, axis=1)


def make_diagonal(coupling, friction, horiz):
    zeros_row = jnp.zeros_like(coupling[:1])
    below = jnp.concatenate([zeros_row, coupling], axis=0)
    above = jnp.concatenate([coupling, zeros_row], axis=0)
    diagonal = 0.5 + 4.0 * horiz[None] + below + above
    return diagonal.at[0].add(friction)


def relax(beside_all, coupling, diagonal, horiz, ice_float, force):
    right_side = horiz * beside_all
    right_side = right_side.at[:, -1].add(force)
    return ice_float * thomas(coupling, diagonal, right_side)


def column_kernel(beside_ref, coupling_ref, friction_ref, horiz_ref, ice_ref, force_ref, out_ref, ratio_ref, partial_ref):
    comps, layers = beside_ref.shape[0], beside_ref.shape[1]
    horiz = horiz_ref[...]
    base = 0.5 + 4.0 * horiz

    def diagonal(level):
        value = base
        if level > 0:
            value = value + coupling_ref[level - 1]
        if level < layers - 1:
            value = value + coupling_ref[level]
        if level == 0:
            value = value + friction_ref[...]
        return value

    def right_side(comp, level):
        value = horiz * beside_ref[comp, level]
        if level == layers - 1:
            value = value + force_ref[comp]
        return value

    pivots = diagonal(0)
    ratio_ref[0] = coupling_ref[0] / pivots
    for comp in range(comps):
        partial_ref[comp, 0] = right_side(comp, 0) / pivots
    for level in range(1, layers):
        below = coupling_ref[level - 1]
        pivots = diagonal(level) - below * ratio_ref[level - 1]
        if level < layers - 1:
            ratio_ref[level] = coupling_ref[level] / pivots
        for comp in range(comps):
            partial_ref[comp, level] = (
                right_side(comp, level) + below * partial_ref[comp, level - 1]
            ) / pivots
    ice = ice_ref[...]
    for comp in range(comps):
        result = partial_ref[comp, layers - 1]
        out_ref[comp, layers - 1] = ice * result
        for level in range(layers - 2, -1, -1):
            result = partial_ref[comp, level] + ratio_ref[level] * result
            out_ref[comp, level] = ice * result


def column_solve(beside, coupling, friction, horiz, ice_float, force):
    comps, layers, rows_x, rows_y = beside.shape
    cells = rows_x * rows_y
    return pl.pallas_call(
        column_kernel,
        out_shape=jax.ShapeDtypeStruct(beside.shape, jnp.float32),
        scratch_shapes=[
            pltpu.VMEM((layers - 1, rows_x, rows_y), jnp.float32),
            pltpu.VMEM(beside.shape, jnp.float32),
        ],
        cost_estimate=pl.CostEstimate(
            flops=12 * comps * layers * cells,
            transcendentals=0,
            bytes_accessed=4 * cells * (2 * comps * layers + layers + 4),
        ),
    )(beside, coupling, friction, horiz, ice_float, force)


def cosine_table(length, after):
    block = 32
    freq = lax.broadcasted_iota(jnp.int32, (1, length), 1)
    freq, _ = lax.optimization_barrier((freq, after))
    coarse = lax.broadcasted_iota(jnp.int32, (length // block, 1), 0)
    fine = lax.broadcasted_iota(jnp.int32, (block, 1), 0)
    period = 4 * length
    scale = jnp.pi / (2.0 * length)
    coarse_angle = ((2 * block * coarse * freq) % period).astype(jnp.float32) * scale
    fine_angle = (((2 * fine + 1) * freq) % period).astype(jnp.float32) * scale
    table = (
        jnp.cos(coarse_angle)[:, None, :] * jnp.cos(fine_angle)[None, :, :]
        - jnp.sin(coarse_angle)[:, None, :] * jnp.sin(fine_angle)[None, :, :]
    ).reshape(length, length)
    norm_factor = jnp.where(freq == 0, jnp.sqrt(1.0 / length), jnp.sqrt(2.0 / length))
    return table * norm_factor.astype(jnp.float32)


def smooth_lines(lines, kappa_val, table):
    length = lines.shape[1]
    modes = lax.iota(jnp.int32, length).astype(jnp.float32)
    spectrum = 1.0 + kappa_val * (2.0 - 2.0 * jnp.cos(jnp.pi * modes / length))
    coefficients = jnp.dot(
        lines, table, precision=lax.Precision.HIGHEST, preferred_element_type=jnp.float32
    )
    coefficients = coefficients / spectrum[None, :]
    return lax.dot_general(
        coefficients,
        table,
        (((1,), (1,)), ((), ())),
        precision=lax.Precision.HIGHEST,
        preferred_element_type=jnp.float32,
    )


def split_parts(value):
    high = lax.reduce_precision(value, exponent_bits=8, mantissa_bits=7)
    rest = value - high
    middle = lax.reduce_precision(rest, exponent_bits=8, mantissa_bits=7)
    low = rest - middle
    return jnp.concatenate([high, middle, low], axis=0).astype(jnp.bfloat16)


def exact_dot(value, selector, contract):
    rows = value.shape[0]
    parts = lax.dot_general(
        split_parts(value),
        selector,
        (((1,), (contract,)), ((), ())),
        preferred_element_type=jnp.float32,
    )
    parts = parts.reshape(3, rows, parts.shape[-1])
    return (parts[0] + parts[1]) + parts[2]


def owner_ranks(owner_hot):
    count, peers = owner_hot.shape
    block = 128
    blocks = count // block
    hot = owner_hot.astype(jnp.bfloat16).reshape(blocks, block, peers)
    lower = (
        lax.broadcasted_iota(jnp.int32, (block, block), 0)
        >= lax.broadcasted_iota(jnp.int32, (block, block), 1)
    ).astype(jnp.bfloat16)
    within = jnp.einsum("ij,bjw->biw", lower, hot, preferred_element_type=jnp.float32)
    totals = within[:, -1, :].astype(jnp.bfloat16)
    strict = (
        lax.broadcasted_iota(jnp.int32, (blocks, blocks), 0)
        > lax.broadcasted_iota(jnp.int32, (blocks, blocks), 1)
    ).astype(jnp.bfloat16)
    before = jnp.dot(strict, totals, preferred_element_type=jnp.float32)
    counts = within + before[:, None, :]
    mine = jnp.where(owner_hot.reshape(blocks, block, peers), counts, 0.0)
    return jnp.sum(mine, axis=-1).reshape(count) - 1.0


def on_device(
    adjoint_start,
    velocity,
    coupling,
    friction,
    horiz,
    ice_mask,
    obs_owner,
    obs_cell,
    obs_value,
    obs_weight,
):
    wide_count = lax.axis_size("wide")
    rows_x, rows_y = friction.shape
    owners = obs_owner[0, :, 0]
    cell_ids = obs_cell[0]
    how_many = owners.shape[0]
    capacity = 2 * how_many // wide_count
    owner_hot = owners[:, None] == jnp.arange(wide_count, dtype=jnp.int32)[None, :]
    ranking = owner_ranks(owner_hot)
    rank_hot = (
        ranking[:, None] == jnp.arange(capacity, dtype=jnp.float32)[None, :]
    ).astype(jnp.bfloat16)
    payload = jnp.stack(
        [obs_value[0, 0], obs_value[1, 0], obs_weight[0], cell_ids.astype(jnp.float32)], axis=0
    )
    spread = jnp.where(owner_hot.T[None, :, :], payload[:, None, :], 0.0)
    packed = exact_dot(spread.reshape(4 * wide_count, how_many), rank_hot, 0)
    packed = packed.reshape(4, wide_count, capacity)
    arrived = lax.all_to_all(packed, "wide", split_axis=1, concat_axis=1, tiled=True).reshape(4, -1)
    target = arrived[3].astype(jnp.int32)
    slots = target.shape[0]
    column_hot = (
        jnp.arange(rows_y, dtype=jnp.int32)[:, None] == (target % rows_y)[None, :]
    ).astype(jnp.bfloat16)
    row_hot = jnp.arange(rows_x, dtype=jnp.int32)[:, None] == (target // rows_y)[None, :]
    top = velocity[:, -1].reshape(2 * rows_x, rows_y)
    picked = exact_dot(top, column_hot, 0).reshape(2, rows_x, slots)
    surface = jnp.sum(jnp.where(row_hot[None], picked, 0.0), axis=1)
    residual = surface - arrived[:2]
    weights = arrived[2]
    weighted = weights * residual
    placed = jnp.where(row_hot[None], weighted[:, None, :], 0.0).reshape(2 * rows_x, slots)
    force = exact_dot(placed, column_hot, 1).reshape(2, rows_x, rows_y)
    local_misfit = 0.5 * jnp.sum(weights * jnp.sum(residual * residual, axis=0))
    ice_float = ice_mask.astype(jnp.float32)
    adjoint = adjoint_start
    for sweep_no in range(ITERS):
        adjoint = column_solve(neighbour_sum(adjoint), coupling, friction, horiz, ice_float, force)
    grad = -friction * ice_float * jnp.sum(adjoint[:, 0] * velocity[:, 0], axis=0)
    misfit_column = jnp.broadcast_to(local_misfit, (rows_y, 1))
    sent = jnp.concatenate([grad.T, misfit_column], axis=1)
    table = cosine_table(wide_count * rows_x, sent)
    lines = lax.all_to_all(sent, "wide", split_axis=0, concat_axis=1, tiled=True)
    width = lines.shape[0]
    lines = lines.reshape(width, wide_count, rows_x + 1)
    wide_misfit = jnp.sum(lines[0, :, rows_x])
    lines = lines[:, :, :rows_x].reshape(width, wide_count * rows_x)
    smooth = smooth_lines(lines, float(KAPPA), table)
    local_square = jnp.sum(smooth * smooth)
    square_column = jnp.broadcast_to(local_square, (width, wide_count, 1))
    returned = jnp.concatenate([smooth.reshape(width, wide_count, rows_x), square_column], axis=2)
    returned = returned.reshape(width, wide_count * (rows_x + 1))
    back = lax.all_to_all(returned, "wide", split_axis=1, concat_axis=0, tiled=True)
    wide_square = jnp.sum(back[::width, rows_x])
    back = back[:, :rows_x].T
    totals = lax.psum(jnp.stack([wide_square, wide_misfit]), "narrow")
    cell_total = wide_count * rows_x * rows_y * lax.axis_size("narrow")
    direction = back * lax.rsqrt(totals[0] / cell_total + 1e-06)
    return (adjoint, direction, totals[1])


def solution(mesh):
    in_specs = (
        P(None, None, "wide", "narrow"),
        P(None, None, "wide", "narrow"),
        P(None, "wide", "narrow"),
        P("wide", "narrow"),
        P("wide", "narrow"),
        P("wide", "narrow"),
        P("narrow", "wide", None),
        P("narrow", "wide"),
        P(None, "narrow", "wide"),
        P("narrow", "wide"),
    )
    out_specs = (P(None, None, "wide", "narrow"), P("wide", "narrow"), P())
    return jax.shard_map(
        on_device, mesh=mesh, in_specs=in_specs, out_specs=out_specs, check_vma=False
    )
```

```python
import jax
import jax.numpy as jnp
from jax import lax
from jax.experimental import pallas as pl
from jax.experimental.pallas import tpu as pltpu
from jax.sharding import PartitionSpec as P

ITERS = 2
KAPPA = 1024


def neighbour_sum(value):
    edges = []
    for axis, dim in (("wide", 2), ("narrow", 3)):
        peers, length = (lax.axis_size(axis), value.shape[dim])
        up = [(i, i + 1) for i in range(peers - 1)]
        down = [(j, i) for i, j in up]
        last = lax.slice_in_dim(value, length - 1, length, axis=dim)
        first = lax.slice_in_dim(value, 0, 1, axis=dim)
        before = lax.ppermute(last, axis, up)
        after = lax.ppermute(first, axis, down)
        inner_next = lax.slice_in_dim(value, 1, length, axis=dim)
        inner_prev = lax.slice_in_dim(value, 0, length - 1, axis=dim)
        edges.append(jnp.concatenate([inner_next, after], axis=dim))
        edges.append(jnp.concatenate([before, inner_prev], axis=dim))
    return edges[0] + edges[1] + edges[2] + edges[3]


def thomas(coupling, diagonal, right_side):
    layers = diagonal.shape[0]
    pivots = diagonal[0]
    ratios = [coupling[0] / pivots]
    partial_sol = [right_side[:, 0] / pivots]
    for level in range(1, layers):
        pivots = diagonal[level] - coupling[level - 1] * ratios[level - 1]
        if level < layers - 1:
            ratios.append(coupling[level] / pivots)
        partial_sol.append(
            (right_side[:, level] + coupling[level - 1] * partial_sol[level - 1]) / pivots
        )
    result = [partial_sol[layers - 1]]
    for level in range(layers - 2, -1, -1):
        result.append(partial_sol[level] + ratios[level] * result[-1])
    ordered = result[::-1]
    return jnp.stack(ordered, axis=1)


def make_diagonal(coupling, friction, horiz):
    zeros_row = jnp.zeros_like(coupling[:1])
    below = jnp.concatenate([zeros_row, coupling], axis=0)
    above = jnp.concatenate([coupling, zeros_row], axis=0)
    diagonal = 0.5 + 4.0 * horiz[None] + below + above
    return diagonal.at[0].add(friction)


def relax(beside_all, coupling, diagonal, horiz, ice_float, force):
    right_side = horiz * beside_all
    right_side = right_side.at[:, -1].add(force)
    return ice_float * thomas(coupling, diagonal, right_side)


def column_kernel(
    adjoint_ref,
    x_prev_ref,
    x_next_ref,
    y_prev_ref,
    y_next_ref,
    coupling_ref,
    friction_ref,
    horiz_ref,
    ice_ref,
    force_ref,
    out_ref,
    ratio_ref,
    partial_ref,
):
    comps, layers, rows_x, rows_y = adjoint_ref.shape
    rows = lax.broadcasted_iota(jnp.int32, (rows_x, rows_y), 0)
    cols = lax.broadcasted_iota(jnp.int32, (rows_x, rows_y), 1)
    horiz = horiz_ref[...]
    base = 0.5 + 4.0 * horiz

    def diagonal(level):
        value = base
        if level > 0:
            value = value + coupling_ref[level - 1]
        if level < layers - 1:
            value = value + coupling_ref[level]
        if level == 0:
            value = value + friction_ref[...]
        return value

    def beside(comp, level):
        center = adjoint_ref[comp, level]
        x_next = jnp.where(rows == rows_x - 1, x_next_ref[comp, level], pltpu.roll(center, rows_x - 1, 0))
        x_prev = jnp.where(rows == 0, x_prev_ref[comp, level], pltpu.roll(center, 1, 0))
        y_next = jnp.where(cols == rows_y - 1, y_next_ref[comp, level], pltpu.roll(center, rows_y - 1, 1))
        y_prev = jnp.where(cols == 0, y_prev_ref[comp, level], pltpu.roll(center, 1, 1))
        return x_next + x_prev + y_next + y_prev

    def right_side(comp, level):
        value = horiz * beside(comp, level)
        if level == layers - 1:
            value = value + force_ref[comp]
        return value

    pivots = diagonal(0)
    ratio_ref[0] = coupling_ref[0] / pivots
    for comp in range(comps):
        partial_ref[comp, 0] = right_side(comp, 0) / pivots
    for level in range(1, layers):
        below = coupling_ref[level - 1]
        pivots = diagonal(level) - below * ratio_ref[level - 1]
        if level < layers - 1:
            ratio_ref[level] = coupling_ref[level] / pivots
        for comp in range(comps):
            partial_ref[comp, level] = (
                right_side(comp, level) + below * partial_ref[comp, level - 1]
            ) / pivots
    ice = ice_ref[...]
    for comp in range(comps):
        result = partial_ref[comp, layers - 1]
        out_ref[comp, layers - 1] = ice * result
        for level in range(layers - 2, -1, -1):
            result = partial_ref[comp, level] + ratio_ref[level] * result
            out_ref[comp, level] = ice * result


def halo_edges(value):
    edges = []
    for axis, dim in (("wide", 2), ("narrow", 3)):
        peers, length = (lax.axis_size(axis), value.shape[dim])
        up = [(i, i + 1) for i in range(peers - 1)]
        down = [(j, i) for i, j in up]
        last = lax.slice_in_dim(value, length - 1, length, axis=dim)
        first = lax.slice_in_dim(value, 0, 1, axis=dim)
        edges.append(lax.ppermute(last, axis, up))
        edges.append(lax.ppermute(first, axis, down))
    return edges


def column_solve(adjoint, edges, coupling, friction, horiz, ice_float, force):
    comps, layers, rows_x, rows_y = adjoint.shape
    cells = rows_x * rows_y
    return pl.pallas_call(
        column_kernel,
        out_shape=jax.ShapeDtypeStruct(adjoint.shape, jnp.float32),
        scratch_shapes=[
            pltpu.VMEM((layers - 1, rows_x, rows_y), jnp.float32),
            pltpu.VMEM(adjoint.shape, jnp.float32),
        ],
        cost_estimate=pl.CostEstimate(
            flops=20 * comps * layers * cells,
            transcendentals=0,
            bytes_accessed=4 * cells * (2 * comps * layers + layers + 4),
        ),
    )(adjoint, *edges, coupling, friction, horiz, ice_float, force)


def cosine_table(length, after):
    block = 32
    freq = lax.broadcasted_iota(jnp.int32, (1, length), 1)
    freq, _ = lax.optimization_barrier((freq, after))
    coarse = lax.broadcasted_iota(jnp.int32, (length // block, 1), 0)
    fine = lax.broadcasted_iota(jnp.int32, (block, 1), 0)
    period = 4 * length
    scale = jnp.pi / (2.0 * length)
    coarse_angle = ((2 * block * coarse * freq) % period).astype(jnp.float32) * scale
    fine_angle = (((2 * fine + 1) * freq) % period).astype(jnp.float32) * scale
    table = (
        jnp.cos(coarse_angle)[:, None, :] * jnp.cos(fine_angle)[None, :, :]
        - jnp.sin(coarse_angle)[:, None, :] * jnp.sin(fine_angle)[None, :, :]
    ).reshape(length, length)
    norm_factor = jnp.where(freq == 0, jnp.sqrt(1.0 / length), jnp.sqrt(2.0 / length))
    return table * norm_factor.astype(jnp.float32)


def smooth_lines(lines, kappa_val, table):
    length = lines.shape[1]
    modes = lax.iota(jnp.int32, length).astype(jnp.float32)
    spectrum = 1.0 + kappa_val * (2.0 - 2.0 * jnp.cos(jnp.pi * modes / length))
    coefficients = jnp.dot(
        lines, table, precision=lax.Precision.HIGHEST, preferred_element_type=jnp.float32
    )
    coefficients = coefficients / spectrum[None, :]
    return lax.dot_general(
        coefficients,
        table,
        (((1,), (1,)), ((), ())),
        precision=lax.Precision.HIGHEST,
        preferred_element_type=jnp.float32,
    )


def split_parts(value):
    high = lax.reduce_precision(value, exponent_bits=8, mantissa_bits=7)
    rest = value - high
    middle = lax.reduce_precision(rest, exponent_bits=8, mantissa_bits=7)
    low = rest - middle
    return jnp.concatenate([high, middle, low], axis=0).astype(jnp.bfloat16)


def exact_dot(value, selector, contract):
    rows = value.shape[0]
    parts = lax.dot_general(
        split_parts(value),
        selector,
        (((1,), (contract,)), ((), ())),
        preferred_element_type=jnp.float32,
    )
    parts = parts.reshape(3, rows, parts.shape[-1])
    return (parts[0] + parts[1]) + parts[2]


def owner_ranks(owner_hot):
    count, peers = owner_hot.shape
    block = 128
    blocks = count // block
    hot = owner_hot.astype(jnp.bfloat16).reshape(blocks, block, peers)
    lower = (
        lax.broadcasted_iota(jnp.int32, (block, block), 0)
        >= lax.broadcasted_iota(jnp.int32, (block, block), 1)
    ).astype(jnp.bfloat16)
    within = jnp.einsum("ij,bjw->biw", lower, hot, preferred_element_type=jnp.float32)
    totals = within[:, -1, :].astype(jnp.bfloat16)
    strict = (
        lax.broadcasted_iota(jnp.int32, (blocks, blocks), 0)
        > lax.broadcasted_iota(jnp.int32, (blocks, blocks), 1)
    ).astype(jnp.bfloat16)
    before = jnp.dot(strict, totals, preferred_element_type=jnp.float32)
    counts = within + before[:, None, :]
    mine = jnp.where(owner_hot.reshape(blocks, block, peers), counts, 0.0)
    return jnp.sum(mine, axis=-1).reshape(count) - 1.0


def on_device(
    adjoint_start,
    velocity,
    coupling,
    friction,
    horiz,
    ice_mask,
    obs_owner,
    obs_cell,
    obs_value,
    obs_weight,
):
    wide_count = lax.axis_size("wide")
    rows_x, rows_y = friction.shape
    owners = obs_owner[0, :, 0]
    cell_ids = obs_cell[0]
    how_many = owners.shape[0]
    capacity = 2 * how_many // wide_count
    owner_hot = owners[:, None] == jnp.arange(wide_count, dtype=jnp.int32)[None, :]
    ranking = owner_ranks(owner_hot)
    rank_hot = (
        ranking[:, None] == jnp.arange(capacity, dtype=jnp.float32)[None, :]
    ).astype(jnp.bfloat16)
    payload = jnp.stack(
        [obs_value[0, 0], obs_value[1, 0], obs_weight[0], cell_ids.astype(jnp.float32)], axis=0
    )
    spread = jnp.where(owner_hot.T[None, :, :], payload[:, None, :], 0.0)
    packed = exact_dot(spread.reshape(4 * wide_count, how_many), rank_hot, 0)
    packed = packed.reshape(4, wide_count, capacity)
    arrived = lax.all_to_all(packed, "wide", split_axis=1, concat_axis=1, tiled=True).reshape(4, -1)
    target = arrived[3].astype(jnp.int32)
    slots = target.shape[0]
    column_hot = (
        jnp.arange(rows_y, dtype=jnp.int32)[:, None] == (target % rows_y)[None, :]
    ).astype(jnp.bfloat16)
    row_hot = jnp.arange(rows_x, dtype=jnp.int32)[:, None] == (target // rows_y)[None, :]
    top = velocity[:, -1].reshape(2 * rows_x, rows_y)
    picked = exact_dot(top, column_hot, 0).reshape(2, rows_x, slots)
    surface = jnp.sum(jnp.where(row_hot[None], picked, 0.0), axis=1)
    residual = surface - arrived[:2]
    weights = arrived[2]
    weighted = weights * residual
    placed = jnp.where(row_hot[None], weighted[:, None, :], 0.0).reshape(2 * rows_x, slots)
    force = exact_dot(placed, column_hot, 1).reshape(2, rows_x, rows_y)
    local_misfit = 0.5 * jnp.sum(weights * jnp.sum(residual * residual, axis=0))
    ice_float = ice_mask.astype(jnp.float32)
    adjoint = adjoint_start
    for sweep_no in range(ITERS):
        adjoint = column_solve(adjoint, halo_edges(adjoint), coupling, friction, horiz, ice_float, force)
    grad = -friction * ice_float * jnp.sum(adjoint[:, 0] * velocity[:, 0], axis=0)
    misfit_column = jnp.broadcast_to(local_misfit, (rows_y, 1))
    sent = jnp.concatenate([grad.T, misfit_column], axis=1)
    table = cosine_table(wide_count * rows_x, sent)
    lines = lax.all_to_all(sent, "wide", split_axis=0, concat_axis=1, tiled=True)
    width = lines.shape[0]
    lines = lines.reshape(width, wide_count, rows_x + 1)
    wide_misfit = jnp.sum(lines[0, :, rows_x])
    lines = lines[:, :, :rows_x].reshape(width, wide_count * rows_x)
    smooth = smooth_lines(lines, float(KAPPA), table)
    local_square = jnp.sum(smooth * smooth)
    square_column = jnp.broadcast_to(local_square, (width, wide_count, 1))
    returned = jnp.concatenate([smooth.reshape(width, wide_count, rows_x), square_column], axis=2)
    returned = returned.reshape(width, wide_count * (rows_x + 1))
    back = lax.all_to_all(returned, "wide", split_axis=1, concat_axis=0, tiled=True)
    wide_square = jnp.sum(back[::width, rows_x])
    back = back[:, :rows_x].T
    totals = lax.psum(jnp.stack([wide_square, wide_misfit]), "narrow")
    cell_total = wide_count * rows_x * rows_y * lax.axis_size("narrow")
    direction = back * lax.rsqrt(totals[0] / cell_total + 1e-06)
    return (adjoint, direction, totals[1])


def solution(mesh):
    in_specs = (
        P(None, None, "wide", "narrow"),
        P(None, None, "wide", "narrow"),
        P(None, "wide", "narrow"),
        P("wide", "narrow"),
        P("wide", "narrow"),
        P("wide", "narrow"),
        P("narrow", "wide", None),
        P("narrow", "wide"),
        P(None, "narrow", "wide"),
        P("narrow", "wide"),
    )
    out_specs = (P(None, None, "wide", "narrow"), P("wide", "narrow"), P())
    return jax.shard_map(
        on_device, mesh=mesh, in_specs=in_specs, out_specs=out_specs, check_vma=False
    )
```

```python
import jax
import jax.numpy as jnp
from jax import lax
from jax.experimental import pallas as pl
from jax.experimental.pallas import tpu as pltpu
from jax.sharding import PartitionSpec as P

ITERS = 2
KAPPA = 1024


def neighbour_sum(value):
    edges = []
    for axis, dim in (("wide", 2), ("narrow", 3)):
        peers, length = (lax.axis_size(axis), value.shape[dim])
        up = [(i, i + 1) for i in range(peers - 1)]
        down = [(j, i) for i, j in up]
        last = lax.slice_in_dim(value, length - 1, length, axis=dim)
        first = lax.slice_in_dim(value, 0, 1, axis=dim)
        before = lax.ppermute(last, axis, up)
        after = lax.ppermute(first, axis, down)
        inner_next = lax.slice_in_dim(value, 1, length, axis=dim)
        inner_prev = lax.slice_in_dim(value, 0, length - 1, axis=dim)
        edges.append(jnp.concatenate([inner_next, after], axis=dim))
        edges.append(jnp.concatenate([before, inner_prev], axis=dim))
    return edges[0] + edges[1] + edges[2] + edges[3]


def thomas(coupling, diagonal, right_side):
    layers = diagonal.shape[0]
    pivots = diagonal[0]
    ratios = [coupling[0] / pivots]
    partial_sol = [right_side[:, 0] / pivots]
    for level in range(1, layers):
        pivots = diagonal[level] - coupling[level - 1] * ratios[level - 1]
        if level < layers - 1:
            ratios.append(coupling[level] / pivots)
        partial_sol.append(
            (right_side[:, level] + coupling[level - 1] * partial_sol[level - 1]) / pivots
        )
    result = [partial_sol[layers - 1]]
    for level in range(layers - 2, -1, -1):
        result.append(partial_sol[level] + ratios[level] * result[-1])
    ordered = result[::-1]
    return jnp.stack(ordered, axis=1)


def make_diagonal(coupling, friction, horiz):
    zeros_row = jnp.zeros_like(coupling[:1])
    below = jnp.concatenate([zeros_row, coupling], axis=0)
    above = jnp.concatenate([coupling, zeros_row], axis=0)
    diagonal = 0.5 + 4.0 * horiz[None] + below + above
    return diagonal.at[0].add(friction)


def relax(beside_all, coupling, diagonal, horiz, ice_float, force):
    right_side = horiz * beside_all
    right_side = right_side.at[:, -1].add(force)
    return ice_float * thomas(coupling, diagonal, right_side)


def column_kernel(
    adjoint_ref,
    x_prev_ref,
    x_next_ref,
    y_prev_ref,
    y_next_ref,
    coupling_ref,
    friction_ref,
    horiz_ref,
    ice_ref,
    force_ref,
    out_ref,
    ratio_ref,
    partial_ref,
):
    comps, layers, rows_x, rows_y = adjoint_ref.shape
    rows = lax.broadcasted_iota(jnp.int32, (rows_x, rows_y), 0)
    cols = lax.broadcasted_iota(jnp.int32, (rows_x, rows_y), 1)
    horiz = horiz_ref[...]
    base = 0.5 + 4.0 * horiz

    def diagonal(level):
        value = base
        if level > 0:
            value = value + coupling_ref[level - 1]
        if level < layers - 1:
            value = value + coupling_ref[level]
        if level == 0:
            value = value + friction_ref[...]
        return value

    def beside(comp, level):
        center = adjoint_ref[comp, level]
        x_next = jnp.where(rows == rows_x - 1, x_next_ref[comp, level], pltpu.roll(center, rows_x - 1, 0))
        x_prev = jnp.where(rows == 0, x_prev_ref[comp, level], pltpu.roll(center, 1, 0))
        y_next = jnp.where(cols == rows_y - 1, y_next_ref[comp, level], pltpu.roll(center, rows_y - 1, 1))
        y_prev = jnp.where(cols == 0, y_prev_ref[comp, level], pltpu.roll(center, 1, 1))
        return x_next + x_prev + y_next + y_prev

    def right_side(comp, level):
        value = horiz * beside(comp, level)
        if level == layers - 1:
            value = value + force_ref[comp]
        return value

    pivots = diagonal(0)
    ratio_ref[0] = coupling_ref[0] / pivots
    for comp in range(comps):
        partial_ref[comp, 0] = right_side(comp, 0) / pivots
    for level in range(1, layers):
        below = coupling_ref[level - 1]
        pivots = diagonal(level) - below * ratio_ref[level - 1]
        if level < layers - 1:
            ratio_ref[level] = coupling_ref[level] / pivots
        for comp in range(comps):
            partial_ref[comp, level] = (
                right_side(comp, level) + below * partial_ref[comp, level - 1]
            ) / pivots
    ice = ice_ref[...]
    for comp in range(comps):
        result = partial_ref[comp, layers - 1]
        out_ref[comp, layers - 1] = ice * result
        for level in range(layers - 2, -1, -1):
            result = partial_ref[comp, level] + ratio_ref[level] * result
            out_ref[comp, level] = ice * result


def halo_edges(value):
    edges = []
    for axis, dim in (("wide", 2), ("narrow", 3)):
        peers, length = (lax.axis_size(axis), value.shape[dim])
        up = [(i, i + 1) for i in range(peers - 1)]
        down = [(j, i) for i, j in up]
        last = lax.slice_in_dim(value, length - 1, length, axis=dim)
        first = lax.slice_in_dim(value, 0, 1, axis=dim)
        edges.append(lax.ppermute(last, axis, up))
        edges.append(lax.ppermute(first, axis, down))
    return edges


def column_solve(adjoint, edges, coupling, friction, horiz, ice_float, force):
    comps, layers, rows_x, rows_y = adjoint.shape
    cells = rows_x * rows_y
    return pl.pallas_call(
        column_kernel,
        out_shape=jax.ShapeDtypeStruct(adjoint.shape, jnp.float32),
        scratch_shapes=[
            pltpu.VMEM((layers - 1, rows_x, rows_y), jnp.float32),
            pltpu.VMEM(adjoint.shape, jnp.float32),
        ],
        cost_estimate=pl.CostEstimate(
            flops=20 * comps * layers * cells,
            transcendentals=0,
            bytes_accessed=4 * cells * (2 * comps * layers + layers + 4),
        ),
    )(adjoint, *edges, coupling, friction, horiz, ice_float, force)


def cosine_table(length, after):
    block = 32
    freq = lax.broadcasted_iota(jnp.int32, (1, length), 1)
    freq, _ = lax.optimization_barrier((freq, after))
    coarse = lax.broadcasted_iota(jnp.int32, (length // block, 1), 0)
    fine = lax.broadcasted_iota(jnp.int32, (block, 1), 0)
    period = 4 * length
    scale = jnp.pi / (2.0 * length)
    coarse_angle = ((2 * block * coarse * freq) % period).astype(jnp.float32) * scale
    fine_angle = (((2 * fine + 1) * freq) % period).astype(jnp.float32) * scale
    table = (
        jnp.cos(coarse_angle)[:, None, :] * jnp.cos(fine_angle)[None, :, :]
        - jnp.sin(coarse_angle)[:, None, :] * jnp.sin(fine_angle)[None, :, :]
    ).reshape(length, length)
    norm_factor = jnp.where(freq == 0, jnp.sqrt(1.0 / length), jnp.sqrt(2.0 / length))
    return table * norm_factor.astype(jnp.float32)


def smooth_lines(lines, kappa_val, table):
    length = lines.shape[1]
    modes = lax.iota(jnp.int32, length).astype(jnp.float32)
    spectrum = 1.0 + kappa_val * (2.0 - 2.0 * jnp.cos(jnp.pi * modes / length))
    coefficients = jnp.dot(
        lines, table, precision=lax.Precision.HIGHEST, preferred_element_type=jnp.float32
    )
    coefficients = coefficients / spectrum[None, :]
    return lax.dot_general(
        coefficients,
        table,
        (((1,), (1,)), ((), ())),
        precision=lax.Precision.HIGHEST,
        preferred_element_type=jnp.float32,
    )


def split_parts(value):
    high = lax.reduce_precision(value, exponent_bits=8, mantissa_bits=7)
    rest = value - high
    middle = lax.reduce_precision(rest, exponent_bits=8, mantissa_bits=7)
    low = rest - middle
    return jnp.concatenate([high, middle, low], axis=0).astype(jnp.bfloat16)


def exact_dot(value, selector, contract):
    rows = value.shape[0]
    parts = lax.dot_general(
        split_parts(value),
        selector,
        (((1,), (contract,)), ((), ())),
        preferred_element_type=jnp.float32,
    )
    parts = parts.reshape(3, rows, parts.shape[-1])
    return (parts[0] + parts[1]) + parts[2]


def owner_ranks(owner_hot):
    count, peers = owner_hot.shape
    block = 128
    blocks = count // block
    hot = owner_hot.astype(jnp.bfloat16).reshape(blocks, block, peers)
    lower = (
        lax.broadcasted_iota(jnp.int32, (block, block), 0)
        >= lax.broadcasted_iota(jnp.int32, (block, block), 1)
    ).astype(jnp.bfloat16)
    within = jnp.einsum("ij,bjw->biw", lower, hot, preferred_element_type=jnp.float32)
    totals = within[:, -1, :].astype(jnp.bfloat16)
    strict = (
        lax.broadcasted_iota(jnp.int32, (blocks, blocks), 0)
        > lax.broadcasted_iota(jnp.int32, (blocks, blocks), 1)
    ).astype(jnp.bfloat16)
    before = jnp.dot(strict, totals, preferred_element_type=jnp.float32)
    counts = within + before[:, None, :]
    mine = jnp.where(owner_hot.reshape(blocks, block, peers), counts, 0.0)
    return jnp.sum(mine, axis=-1).reshape(count) - 1.0


def on_device(
    adjoint_start,
    velocity,
    coupling,
    friction,
    horiz,
    ice_mask,
    obs_owner,
    obs_cell,
    obs_value,
    obs_weight,
):
    wide_count = lax.axis_size("wide")
    rows_x, rows_y = friction.shape
    owners = obs_owner[0, :, 0]
    cell_ids = obs_cell[0]
    how_many = owners.shape[0]
    capacity = 2 * how_many // wide_count
    owner_hot = owners[:, None] == jnp.arange(wide_count, dtype=jnp.int32)[None, :]
    ranking = owner_ranks(owner_hot)
    rank_hot = (
        ranking[:, None] == jnp.arange(capacity, dtype=jnp.float32)[None, :]
    ).astype(jnp.bfloat16)
    payload = jnp.stack(
        [obs_value[0, 0], obs_value[1, 0], obs_weight[0], cell_ids.astype(jnp.float32)], axis=0
    )
    spread = jnp.where(owner_hot.T[None, :, :], payload[:, None, :], 0.0)
    packed = exact_dot(spread.reshape(4 * wide_count, how_many), rank_hot, 0)
    packed = packed.reshape(4, wide_count, capacity)
    arrived = lax.all_to_all(packed, "wide", split_axis=1, concat_axis=1, tiled=True).reshape(4, -1)
    adjoint, arrived = lax.optimization_barrier((adjoint_start, arrived))
    target = arrived[3].astype(jnp.int32)
    slots = target.shape[0]
    column_hot = (
        jnp.arange(rows_y, dtype=jnp.int32)[:, None] == (target % rows_y)[None, :]
    ).astype(jnp.bfloat16)
    row_hot = jnp.arange(rows_x, dtype=jnp.int32)[:, None] == (target // rows_y)[None, :]
    top = velocity[:, -1].reshape(2 * rows_x, rows_y)
    picked = exact_dot(top, column_hot, 0).reshape(2, rows_x, slots)
    surface = jnp.sum(jnp.where(row_hot[None], picked, 0.0), axis=1)
    residual = surface - arrived[:2]
    weights = arrived[2]
    weighted = weights * residual
    placed = jnp.where(row_hot[None], weighted[:, None, :], 0.0).reshape(2 * rows_x, slots)
    force = exact_dot(placed, column_hot, 1).reshape(2, rows_x, rows_y)
    local_misfit = 0.5 * jnp.sum(weights * jnp.sum(residual * residual, axis=0))
    ice_float = ice_mask.astype(jnp.float32)
    for sweep_no in range(ITERS):
        adjoint = column_solve(adjoint, halo_edges(adjoint), coupling, friction, horiz, ice_float, force)
    grad = -friction * ice_float * jnp.sum(adjoint[:, 0] * velocity[:, 0], axis=0)
    misfit_column = jnp.broadcast_to(local_misfit, (rows_y, 1))
    sent = jnp.concatenate([grad.T, misfit_column], axis=1)
    table = cosine_table(wide_count * rows_x, sent)
    lines = lax.all_to_all(sent, "wide", split_axis=0, concat_axis=1, tiled=True)
    width = lines.shape[0]
    lines = lines.reshape(width, wide_count, rows_x + 1)
    wide_misfit = jnp.sum(lines[0, :, rows_x])
    lines = lines[:, :, :rows_x].reshape(width, wide_count * rows_x)
    smooth = smooth_lines(lines, float(KAPPA), table)
    local_square = jnp.sum(smooth * smooth)
    square_column = jnp.broadcast_to(local_square, (width, wide_count, 1))
    returned = jnp.concatenate([smooth.reshape(width, wide_count, rows_x), square_column], axis=2)
    returned = returned.reshape(width, wide_count * (rows_x + 1))
    back = lax.all_to_all(returned, "wide", split_axis=1, concat_axis=0, tiled=True)
    wide_square = jnp.sum(back[::width, rows_x])
    back = back[:, :rows_x].T
    totals = lax.psum(jnp.stack([wide_square, wide_misfit]), "narrow")
    cell_total = wide_count * rows_x * rows_y * lax.axis_size("narrow")
    direction = back * lax.rsqrt(totals[0] / cell_total + 1e-06)
    return (adjoint, direction, totals[1])


def solution(mesh):
    in_specs = (
        P(None, None, "wide", "narrow"),
        P(None, None, "wide", "narrow"),
        P(None, "wide", "narrow"),
        P("wide", "narrow"),
        P("wide", "narrow"),
        P("wide", "narrow"),
        P("narrow", "wide", None),
        P("narrow", "wide"),
        P(None, "narrow", "wide"),
        P("narrow", "wide"),
    )
    out_specs = (P(None, None, "wide", "narrow"), P("wide", "narrow"), P())
    return jax.shard_map(
        on_device, mesh=mesh, in_specs=in_specs, out_specs=out_specs, check_vma=False
    )
```

```python
import jax
import jax.numpy as jnp
from jax import lax
from jax.experimental import pallas as pl
from jax.experimental.pallas import tpu as pltpu
from jax.sharding import PartitionSpec as P

ITERS = 2
KAPPA = 1024


def neighbour_sum(value):
    edges = []
    for axis, dim in (("wide", 2), ("narrow", 3)):
        peers, length = (lax.axis_size(axis), value.shape[dim])
        up = [(i, i + 1) for i in range(peers - 1)]
        down = [(j, i) for i, j in up]
        last = lax.slice_in_dim(value, length - 1, length, axis=dim)
        first = lax.slice_in_dim(value, 0, 1, axis=dim)
        before = lax.ppermute(last, axis, up)
        after = lax.ppermute(first, axis, down)
        inner_next = lax.slice_in_dim(value, 1, length, axis=dim)
        inner_prev = lax.slice_in_dim(value, 0, length - 1, axis=dim)
        edges.append(jnp.concatenate([inner_next, after], axis=dim))
        edges.append(jnp.concatenate([before, inner_prev], axis=dim))
    return edges[0] + edges[1] + edges[2] + edges[3]


def thomas(coupling, diagonal, right_side):
    layers = diagonal.shape[0]
    pivots = diagonal[0]
    ratios = [coupling[0] / pivots]
    partial_sol = [right_side[:, 0] / pivots]
    for level in range(1, layers):
        pivots = diagonal[level] - coupling[level - 1] * ratios[level - 1]
        if level < layers - 1:
            ratios.append(coupling[level] / pivots)
        partial_sol.append(
            (right_side[:, level] + coupling[level - 1] * partial_sol[level - 1]) / pivots
        )
    result = [partial_sol[layers - 1]]
    for level in range(layers - 2, -1, -1):
        result.append(partial_sol[level] + ratios[level] * result[-1])
    ordered = result[::-1]
    return jnp.stack(ordered, axis=1)


def make_diagonal(coupling, friction, horiz):
    zeros_row = jnp.zeros_like(coupling[:1])
    below = jnp.concatenate([zeros_row, coupling], axis=0)
    above = jnp.concatenate([coupling, zeros_row], axis=0)
    diagonal = 0.5 + 4.0 * horiz[None] + below + above
    return diagonal.at[0].add(friction)


def relax(beside_all, coupling, diagonal, horiz, ice_float, force):
    right_side = horiz * beside_all
    right_side = right_side.at[:, -1].add(force)
    return ice_float * thomas(coupling, diagonal, right_side)


def column_kernel(
    adjoint_ref,
    x_prev_ref,
    x_next_ref,
    y_prev_ref,
    y_next_ref,
    coupling_ref,
    friction_ref,
    horiz_ref,
    ice_ref,
    force_ref,
    out_ref,
    ratio_ref,
    partial_ref,
):
    comps, layers, rows_x, rows_y = adjoint_ref.shape
    rows = lax.broadcasted_iota(jnp.int32, (rows_x, rows_y), 0)
    cols = lax.broadcasted_iota(jnp.int32, (rows_x, rows_y), 1)
    horiz = horiz_ref[...]
    base = 0.5 + 4.0 * horiz

    def diagonal(level):
        value = base
        if level > 0:
            value = value + coupling_ref[level - 1]
        if level < layers - 1:
            value = value + coupling_ref[level]
        if level == 0:
            value = value + friction_ref[...]
        return value

    def beside(comp, level):
        center = adjoint_ref[comp, level]
        x_next = jnp.where(rows == rows_x - 1, x_next_ref[comp, level], pltpu.roll(center, rows_x - 1, 0))
        x_prev = jnp.where(rows == 0, x_prev_ref[comp, level], pltpu.roll(center, 1, 0))
        y_next = jnp.where(cols == rows_y - 1, y_next_ref[comp, level], pltpu.roll(center, rows_y - 1, 1))
        y_prev = jnp.where(cols == 0, y_prev_ref[comp, level], pltpu.roll(center, 1, 1))
        return x_next + x_prev + y_next + y_prev

    def right_side(comp, level):
        value = horiz * beside(comp, level)
        if level == layers - 1:
            value = value + force_ref[comp]
        return value

    pivots = diagonal(0)
    ratio_ref[0] = coupling_ref[0] / pivots
    for comp in range(comps):
        partial_ref[comp, 0] = right_side(comp, 0) / pivots
    for level in range(1, layers):
        below = coupling_ref[level - 1]
        pivots = diagonal(level) - below * ratio_ref[level - 1]
        if level < layers - 1:
            ratio_ref[level] = coupling_ref[level] / pivots
        for comp in range(comps):
            partial_ref[comp, level] = (
                right_side(comp, level) + below * partial_ref[comp, level - 1]
            ) / pivots
    ice = ice_ref[...]
    for comp in range(comps):
        result = partial_ref[comp, layers - 1]
        out_ref[comp, layers - 1] = ice * result
        for level in range(layers - 2, -1, -1):
            result = partial_ref[comp, level] + ratio_ref[level] * result
            out_ref[comp, level] = ice * result


def halo_edges(value):
    edges = []
    for axis, dim in (("wide", 2), ("narrow", 3)):
        peers, length = (lax.axis_size(axis), value.shape[dim])
        up = [(i, i + 1) for i in range(peers - 1)]
        down = [(j, i) for i, j in up]
        last = lax.slice_in_dim(value, length - 1, length, axis=dim)
        first = lax.slice_in_dim(value, 0, 1, axis=dim)
        edges.append(lax.ppermute(last, axis, up))
        edges.append(lax.ppermute(first, axis, down))
    return edges


def column_solve(adjoint, edges, coupling, friction, horiz, ice_float, force):
    comps, layers, rows_x, rows_y = adjoint.shape
    cells = rows_x * rows_y
    return pl.pallas_call(
        column_kernel,
        out_shape=jax.ShapeDtypeStruct(adjoint.shape, jnp.float32),
        scratch_shapes=[
            pltpu.VMEM((layers - 1, rows_x, rows_y), jnp.float32),
            pltpu.VMEM(adjoint.shape, jnp.float32),
        ],
        cost_estimate=pl.CostEstimate(
            flops=20 * comps * layers * cells,
            transcendentals=0,
            bytes_accessed=4 * cells * (2 * comps * layers + layers + 4),
        ),
    )(adjoint, *edges, coupling, friction, horiz, ice_float, force)


def cosine_table(length):
    block = 32
    freq = lax.broadcasted_iota(jnp.int32, (1, length), 1)
    coarse = lax.broadcasted_iota(jnp.int32, (length // block, 1), 0)
    fine = lax.broadcasted_iota(jnp.int32, (block, 1), 0)
    period = 4 * length
    scale = jnp.pi / (2.0 * length)
    coarse_angle = ((2 * block * coarse * freq) % period).astype(jnp.float32) * scale
    fine_angle = (((2 * fine + 1) * freq) % period).astype(jnp.float32) * scale
    table = (
        jnp.cos(coarse_angle)[:, None, :] * jnp.cos(fine_angle)[None, :, :]
        - jnp.sin(coarse_angle)[:, None, :] * jnp.sin(fine_angle)[None, :, :]
    ).reshape(length, length)
    norm_factor = jnp.where(freq == 0, jnp.sqrt(1.0 / length), jnp.sqrt(2.0 / length))
    return table * norm_factor.astype(jnp.float32)


def smooth_lines(lines, kappa_val, table):
    length = lines.shape[1]
    modes = lax.iota(jnp.int32, length).astype(jnp.float32)
    spectrum = 1.0 + kappa_val * (2.0 - 2.0 * jnp.cos(jnp.pi * modes / length))
    coefficients = jnp.dot(
        lines, table, precision=lax.Precision.HIGHEST, preferred_element_type=jnp.float32
    )
    coefficients = coefficients / spectrum[None, :]
    return lax.dot_general(
        coefficients,
        table,
        (((1,), (1,)), ((), ())),
        precision=lax.Precision.HIGHEST,
        preferred_element_type=jnp.float32,
    )


def split_parts(value):
    high = lax.reduce_precision(value, exponent_bits=8, mantissa_bits=7)
    rest = value - high
    middle = lax.reduce_precision(rest, exponent_bits=8, mantissa_bits=7)
    low = rest - middle
    return jnp.concatenate([high, middle, low], axis=0).astype(jnp.bfloat16)


def exact_dot(value, selector, contract):
    rows = value.shape[0]
    parts = lax.dot_general(
        split_parts(value),
        selector,
        (((1,), (contract,)), ((), ())),
        preferred_element_type=jnp.float32,
    )
    parts = parts.reshape(3, rows, parts.shape[-1])
    return (parts[0] + parts[1]) + parts[2]


def owner_ranks(owner_hot):
    count, peers = owner_hot.shape
    block = 128
    blocks = count // block
    hot = owner_hot.astype(jnp.bfloat16).reshape(blocks, block, peers)
    lower = (
        lax.broadcasted_iota(jnp.int32, (block, block), 0)
        >= lax.broadcasted_iota(jnp.int32, (block, block), 1)
    ).astype(jnp.bfloat16)
    within = jnp.einsum("ij,bjw->biw", lower, hot, preferred_element_type=jnp.float32)
    totals = within[:, -1, :].astype(jnp.bfloat16)
    strict = (
        lax.broadcasted_iota(jnp.int32, (blocks, blocks), 0)
        > lax.broadcasted_iota(jnp.int32, (blocks, blocks), 1)
    ).astype(jnp.bfloat16)
    before = jnp.dot(strict, totals, preferred_element_type=jnp.float32)
    counts = within + before[:, None, :]
    mine = jnp.where(owner_hot.reshape(blocks, block, peers), counts, 0.0)
    return jnp.sum(mine, axis=-1).reshape(count) - 1.0


def on_device(
    adjoint_start,
    velocity,
    coupling,
    friction,
    horiz,
    ice_mask,
    obs_owner,
    obs_cell,
    obs_value,
    obs_weight,
):
    wide_count = lax.axis_size("wide")
    rows_x, rows_y = friction.shape
    owners = obs_owner[0, :, 0]
    cell_ids = obs_cell[0]
    how_many = owners.shape[0]
    capacity = 2 * how_many // wide_count
    owner_hot = owners[:, None] == jnp.arange(wide_count, dtype=jnp.int32)[None, :]
    ranking = owner_ranks(owner_hot)
    rank_hot = (
        ranking[:, None] == jnp.arange(capacity, dtype=jnp.float32)[None, :]
    ).astype(jnp.bfloat16)
    payload = jnp.stack(
        [obs_value[0, 0], obs_value[1, 0], obs_weight[0], cell_ids.astype(jnp.float32)], axis=0
    )
    spread = jnp.where(owner_hot.T[None, :, :], payload[:, None, :], 0.0)
    packed = exact_dot(spread.reshape(4 * wide_count, how_many), rank_hot, 0)
    packed = packed.reshape(4, wide_count, capacity)
    arrived = lax.all_to_all(packed, "wide", split_axis=1, concat_axis=1, tiled=True).reshape(4, -1)
    target = arrived[3].astype(jnp.int32)
    slots = target.shape[0]
    column_hot = (
        jnp.arange(rows_y, dtype=jnp.int32)[:, None] == (target % rows_y)[None, :]
    ).astype(jnp.bfloat16)
    row_hot = jnp.arange(rows_x, dtype=jnp.int32)[:, None] == (target // rows_y)[None, :]
    top = velocity[:, -1].reshape(2 * rows_x, rows_y)
    picked = exact_dot(top, column_hot, 0).reshape(2, rows_x, slots)
    surface = jnp.sum(jnp.where(row_hot[None], picked, 0.0), axis=1)
    residual = surface - arrived[:2]
    weights = arrived[2]
    weighted = weights * residual
    placed = jnp.where(row_hot[None], weighted[:, None, :], 0.0).reshape(2 * rows_x, slots)
    force = exact_dot(placed, column_hot, 1).reshape(2, rows_x, rows_y)
    local_misfit = 0.5 * jnp.sum(weights * jnp.sum(residual * residual, axis=0))
    ice_float = ice_mask.astype(jnp.float32)
    adjoint = adjoint_start
    for sweep_no in range(ITERS):
        adjoint = column_solve(adjoint, halo_edges(adjoint), coupling, friction, horiz, ice_float, force)
    grad = -friction * ice_float * jnp.sum(adjoint[:, 0] * velocity[:, 0], axis=0)
    misfit_column = jnp.broadcast_to(local_misfit, (rows_y, 1))
    sent = jnp.concatenate([grad.T, misfit_column], axis=1)
    table = cosine_table(wide_count * rows_x)
    lines = lax.all_to_all(sent, "wide", split_axis=0, concat_axis=1, tiled=True)
    width = lines.shape[0]
    lines = lines.reshape(width, wide_count, rows_x + 1)
    wide_misfit = jnp.sum(lines[0, :, rows_x])
    lines = lines[:, :, :rows_x].reshape(width, wide_count * rows_x)
    smooth = smooth_lines(lines, float(KAPPA), table)
    local_square = jnp.sum(smooth * smooth)
    square_column = jnp.broadcast_to(local_square, (width, wide_count, 1))
    returned = jnp.concatenate([smooth.reshape(width, wide_count, rows_x), square_column], axis=2)
    returned = returned.reshape(width, wide_count * (rows_x + 1))
    back = lax.all_to_all(returned, "wide", split_axis=1, concat_axis=0, tiled=True)
    wide_square = jnp.sum(back[::width, rows_x])
    back = back[:, :rows_x].T
    totals = lax.psum(jnp.stack([wide_square, wide_misfit]), "narrow")
    cell_total = wide_count * rows_x * rows_y * lax.axis_size("narrow")
    direction = back * lax.rsqrt(totals[0] / cell_total + 1e-06)
    return (adjoint, direction, totals[1])


def solution(mesh):
    in_specs = (
        P(None, None, "wide", "narrow"),
        P(None, None, "wide", "narrow"),
        P(None, "wide", "narrow"),
        P("wide", "narrow"),
        P("wide", "narrow"),
        P("wide", "narrow"),
        P("narrow", "wide", None),
        P("narrow", "wide"),
        P(None, "narrow", "wide"),
        P("narrow", "wide"),
    )
    out_specs = (P(None, None, "wide", "narrow"), P("wide", "narrow"), P())
    return jax.shard_map(
        on_device, mesh=mesh, in_specs=in_specs, out_specs=out_specs, check_vma=False
    )
```

```python
import jax
import jax.numpy as jnp
from jax import lax
from jax.experimental import pallas as pl
from jax.experimental.pallas import tpu as pltpu
from jax.sharding import PartitionSpec as P

ITERS = 2
KAPPA = 1024


def neighbour_sum(value):
    edges = []
    for axis, dim in (("wide", 2), ("narrow", 3)):
        peers, length = (lax.axis_size(axis), value.shape[dim])
        up = [(i, i + 1) for i in range(peers - 1)]
        down = [(j, i) for i, j in up]
        last = lax.slice_in_dim(value, length - 1, length, axis=dim)
        first = lax.slice_in_dim(value, 0, 1, axis=dim)
        before = lax.ppermute(last, axis, up)
        after = lax.ppermute(first, axis, down)
        inner_next = lax.slice_in_dim(value, 1, length, axis=dim)
        inner_prev = lax.slice_in_dim(value, 0, length - 1, axis=dim)
        edges.append(jnp.concatenate([inner_next, after], axis=dim))
        edges.append(jnp.concatenate([before, inner_prev], axis=dim))
    return edges[0] + edges[1] + edges[2] + edges[3]


def thomas(coupling, diagonal, right_side):
    layers = diagonal.shape[0]
    pivots = diagonal[0]
    ratios = [coupling[0] / pivots]
    partial_sol = [right_side[:, 0] / pivots]
    for level in range(1, layers):
        pivots = diagonal[level] - coupling[level - 1] * ratios[level - 1]
        if level < layers - 1:
            ratios.append(coupling[level] / pivots)
        partial_sol.append(
            (right_side[:, level] + coupling[level - 1] * partial_sol[level - 1]) / pivots
        )
    result = [partial_sol[layers - 1]]
    for level in range(layers - 2, -1, -1):
        result.append(partial_sol[level] + ratios[level] * result[-1])
    ordered = result[::-1]
    return jnp.stack(ordered, axis=1)


def make_diagonal(coupling, friction, horiz):
    zeros_row = jnp.zeros_like(coupling[:1])
    below = jnp.concatenate([zeros_row, coupling], axis=0)
    above = jnp.concatenate([coupling, zeros_row], axis=0)
    diagonal = 0.5 + 4.0 * horiz[None] + below + above
    return diagonal.at[0].add(friction)


def relax(beside_all, coupling, diagonal, horiz, ice_float, force):
    right_side = horiz * beside_all
    right_side = right_side.at[:, -1].add(force)
    return ice_float * thomas(coupling, diagonal, right_side)


def column_kernel(
    adjoint_ref,
    x_prev_ref,
    x_next_ref,
    y_prev_ref,
    y_next_ref,
    coupling_ref,
    friction_ref,
    horiz_ref,
    ice_ref,
    force_ref,
    out_ref,
    *rest,
):
    edge_refs, (ratio_ref, partial_ref) = rest[:-2], rest[-2:]
    comps, layers, rows_x, rows_y = adjoint_ref.shape
    rows = lax.broadcasted_iota(jnp.int32, (rows_x, rows_y), 0)
    cols = lax.broadcasted_iota(jnp.int32, (rows_x, rows_y), 1)
    horiz = horiz_ref[...]
    base = 0.5 + 4.0 * horiz

    def diagonal(level):
        value = base
        if level > 0:
            value = value + coupling_ref[level - 1]
        if level < layers - 1:
            value = value + coupling_ref[level]
        if level == 0:
            value = value + friction_ref[...]
        return value

    def beside(comp, level):
        center = adjoint_ref[comp, level]
        x_next = jnp.where(rows == rows_x - 1, x_next_ref[comp, level], pltpu.roll(center, rows_x - 1, 0))
        x_prev = jnp.where(rows == 0, x_prev_ref[comp, level], pltpu.roll(center, 1, 0))
        y_next = jnp.where(cols == rows_y - 1, y_next_ref[comp, level], pltpu.roll(center, rows_y - 1, 1))
        y_prev = jnp.where(cols == 0, y_prev_ref[comp, level], pltpu.roll(center, 1, 1))
        return x_next + x_prev + y_next + y_prev

    def right_side(comp, level):
        value = horiz * beside(comp, level)
        if level == layers - 1:
            value = value + force_ref[comp]
        return value

    pivots = diagonal(0)
    ratio_ref[0] = coupling_ref[0] / pivots
    for comp in range(comps):
        partial_ref[comp, 0] = right_side(comp, 0) / pivots
    for level in range(1, layers):
        below = coupling_ref[level - 1]
        pivots = diagonal(level) - below * ratio_ref[level - 1]
        if level < layers - 1:
            ratio_ref[level] = coupling_ref[level] / pivots
        for comp in range(comps):
            partial_ref[comp, level] = (
                right_side(comp, level) + below * partial_ref[comp, level - 1]
            ) / pivots
    ice = ice_ref[...]
    for comp in range(comps):
        result = partial_ref[comp, layers - 1]
        out_ref[comp, layers - 1] = ice * result
        for level in range(layers - 2, -1, -1):
            result = partial_ref[comp, level] + ratio_ref[level] * result
            out_ref[comp, level] = ice * result
    if edge_refs:
        last_row, first_row, last_col, first_col = edge_refs
        last_row[...] = out_ref[:, :, rows_x - 1 : rows_x, :]
        first_row[...] = out_ref[:, :, 0:1, :]
        for comp in range(comps):
            for level in range(layers):
                last_col[comp, level] = out_ref[comp, level, :, rows_y - 128 : rows_y][:, 127:128]
                first_col[comp, level] = out_ref[comp, level, :, 0:128][:, 0:1]


def block_edges(value):
    edges = []
    for dim in (2, 3):
        length = value.shape[dim]
        edges.append(lax.slice_in_dim(value, length - 1, length, axis=dim))
        edges.append(lax.slice_in_dim(value, 0, 1, axis=dim))
    return edges


def halo_edges(block):
    edges = []
    for index, axis in enumerate(("wide", "narrow")):
        peers = lax.axis_size(axis)
        up = [(i, i + 1) for i in range(peers - 1)]
        down = [(j, i) for i, j in up]
        edges.append(lax.ppermute(block[2 * index], axis, up))
        edges.append(lax.ppermute(block[2 * index + 1], axis, down))
    return edges


def column_solve(adjoint, edges, coupling, friction, horiz, ice_float, force, with_edges):
    comps, layers, rows_x, rows_y = adjoint.shape
    cells = rows_x * rows_y
    out_shape = jax.ShapeDtypeStruct(adjoint.shape, jnp.float32)
    if with_edges:
        row = jax.ShapeDtypeStruct((comps, layers, 1, rows_y), jnp.float32)
        col = jax.ShapeDtypeStruct((comps, layers, rows_x, 1), jnp.float32)
        out_shape = (out_shape, row, row, col, col)
    return pl.pallas_call(
        column_kernel,
        out_shape=out_shape,
        scratch_shapes=[
            pltpu.VMEM((layers - 1, rows_x, rows_y), jnp.float32),
            pltpu.VMEM(adjoint.shape, jnp.float32),
        ],
        cost_estimate=pl.CostEstimate(
            flops=20 * comps * layers * cells,
            transcendentals=0,
            bytes_accessed=4 * cells * (2 * comps * layers + layers + 4),
        ),
    )(adjoint, *edges, coupling, friction, horiz, ice_float, force)


def cosine_table(length, after):
    block = 32
    freq = lax.broadcasted_iota(jnp.int32, (1, length), 1)
    freq, _ = lax.optimization_barrier((freq, after))
    coarse = lax.broadcasted_iota(jnp.int32, (length // block, 1), 0)
    fine = lax.broadcasted_iota(jnp.int32, (block, 1), 0)
    period = 4 * length
    scale = jnp.pi / (2.0 * length)
    coarse_angle = ((2 * block * coarse * freq) % period).astype(jnp.float32) * scale
    fine_angle = (((2 * fine + 1) * freq) % period).astype(jnp.float32) * scale
    table = (
        jnp.cos(coarse_angle)[:, None, :] * jnp.cos(fine_angle)[None, :, :]
        - jnp.sin(coarse_angle)[:, None, :] * jnp.sin(fine_angle)[None, :, :]
    ).reshape(length, length)
    norm_factor = jnp.where(freq == 0, jnp.sqrt(1.0 / length), jnp.sqrt(2.0 / length))
    return table * norm_factor.astype(jnp.float32)


def smooth_lines(lines, kappa_val, table):
    length = lines.shape[1]
    modes = lax.iota(jnp.int32, length).astype(jnp.float32)
    spectrum = 1.0 + kappa_val * (2.0 - 2.0 * jnp.cos(jnp.pi * modes / length))
    coefficients = jnp.dot(
        lines, table, precision=lax.Precision.HIGHEST, preferred_element_type=jnp.float32
    )
    coefficients = coefficients / spectrum[None, :]
    return lax.dot_general(
        coefficients,
        table,
        (((1,), (1,)), ((), ())),
        precision=lax.Precision.HIGHEST,
        preferred_element_type=jnp.float32,
    )


def split_parts(value):
    high = lax.reduce_precision(value, exponent_bits=8, mantissa_bits=7)
    rest = value - high
    middle = lax.reduce_precision(rest, exponent_bits=8, mantissa_bits=7)
    low = rest - middle
    return jnp.concatenate([high, middle, low], axis=0).astype(jnp.bfloat16)


def exact_dot(value, selector, contract):
    rows = value.shape[0]
    parts = lax.dot_general(
        split_parts(value),
        selector,
        (((1,), (contract,)), ((), ())),
        preferred_element_type=jnp.float32,
    )
    parts = parts.reshape(3, rows, parts.shape[-1])
    return (parts[0] + parts[1]) + parts[2]


def owner_ranks(owner_hot):
    count, peers = owner_hot.shape
    block = 128
    blocks = count // block
    hot = owner_hot.astype(jnp.bfloat16).reshape(blocks, block, peers)
    lower = (
        lax.broadcasted_iota(jnp.int32, (block, block), 0)
        >= lax.broadcasted_iota(jnp.int32, (block, block), 1)
    ).astype(jnp.bfloat16)
    within = jnp.einsum("ij,bjw->biw", lower, hot, preferred_element_type=jnp.float32)
    totals = within[:, -1, :].astype(jnp.bfloat16)
    strict = (
        lax.broadcasted_iota(jnp.int32, (blocks, blocks), 0)
        > lax.broadcasted_iota(jnp.int32, (blocks, blocks), 1)
    ).astype(jnp.bfloat16)
    before = jnp.dot(strict, totals, preferred_element_type=jnp.float32)
    counts = within + before[:, None, :]
    mine = jnp.where(owner_hot.reshape(blocks, block, peers), counts, 0.0)
    return jnp.sum(mine, axis=-1).reshape(count) - 1.0


def on_device(
    adjoint_start,
    velocity,
    coupling,
    friction,
    horiz,
    ice_mask,
    obs_owner,
    obs_cell,
    obs_value,
    obs_weight,
):
    wide_count = lax.axis_size("wide")
    rows_x, rows_y = friction.shape
    owners = obs_owner[0, :, 0]
    cell_ids = obs_cell[0]
    how_many = owners.shape[0]
    capacity = 2 * how_many // wide_count
    owner_hot = owners[:, None] == jnp.arange(wide_count, dtype=jnp.int32)[None, :]
    ranking = owner_ranks(owner_hot)
    rank_hot = (
        ranking[:, None] == jnp.arange(capacity, dtype=jnp.float32)[None, :]
    ).astype(jnp.bfloat16)
    payload = jnp.stack(
        [obs_value[0, 0], obs_value[1, 0], obs_weight[0], cell_ids.astype(jnp.float32)], axis=0
    )
    spread = jnp.where(owner_hot.T[None, :, :], payload[:, None, :], 0.0)
    packed = exact_dot(spread.reshape(4 * wide_count, how_many), rank_hot, 0)
    packed = packed.reshape(4, wide_count, capacity)
    arrived = lax.all_to_all(packed, "wide", split_axis=1, concat_axis=1, tiled=True).reshape(4, -1)
    target = arrived[3].astype(jnp.int32)
    slots = target.shape[0]
    column_hot = (
        jnp.arange(rows_y, dtype=jnp.int32)[:, None] == (target % rows_y)[None, :]
    ).astype(jnp.bfloat16)
    row_hot = jnp.arange(rows_x, dtype=jnp.int32)[:, None] == (target // rows_y)[None, :]
    top = velocity[:, -1].reshape(2 * rows_x, rows_y)
    picked = exact_dot(top, column_hot, 0).reshape(2, rows_x, slots)
    surface = jnp.sum(jnp.where(row_hot[None], picked, 0.0), axis=1)
    residual = surface - arrived[:2]
    weights = arrived[2]
    weighted = weights * residual
    placed = jnp.where(row_hot[None], weighted[:, None, :], 0.0).reshape(2 * rows_x, slots)
    force = exact_dot(placed, column_hot, 1).reshape(2, rows_x, rows_y)
    local_misfit = 0.5 * jnp.sum(weights * jnp.sum(residual * residual, axis=0))
    ice_float = ice_mask.astype(jnp.float32)
    adjoint = adjoint_start
    block = block_edges(adjoint)
    for sweep_no in range(ITERS):
        solved = column_solve(
            adjoint, halo_edges(block), coupling, friction, horiz, ice_float, force,
            sweep_no < ITERS - 1,
        )
        if sweep_no < ITERS - 1:
            adjoint, block = solved[0], list(solved[1:])
        else:
            adjoint = solved
    grad = -friction * ice_float * jnp.sum(adjoint[:, 0] * velocity[:, 0], axis=0)
    misfit_column = jnp.broadcast_to(local_misfit, (rows_y, 1))
    sent = jnp.concatenate([grad.T, misfit_column], axis=1)
    table = cosine_table(wide_count * rows_x, sent)
    lines = lax.all_to_all(sent, "wide", split_axis=0, concat_axis=1, tiled=True)
    width = lines.shape[0]
    lines = lines.reshape(width, wide_count, rows_x + 1)
    wide_misfit = jnp.sum(lines[0, :, rows_x])
    lines = lines[:, :, :rows_x].reshape(width, wide_count * rows_x)
    smooth = smooth_lines(lines, float(KAPPA), table)
    local_square = jnp.sum(smooth * smooth)
    square_column = jnp.broadcast_to(local_square, (width, wide_count, 1))
    returned = jnp.concatenate([smooth.reshape(width, wide_count, rows_x), square_column], axis=2)
    returned = returned.reshape(width, wide_count * (rows_x + 1))
    back = lax.all_to_all(returned, "wide", split_axis=1, concat_axis=0, tiled=True)
    wide_square = jnp.sum(back[::width, rows_x])
    back = back[:, :rows_x].T
    totals = lax.psum(jnp.stack([wide_square, wide_misfit]), "narrow")
    cell_total = wide_count * rows_x * rows_y * lax.axis_size("narrow")
    direction = back * lax.rsqrt(totals[0] / cell_total + 1e-06)
    return (adjoint, direction, totals[1])


def solution(mesh):
    in_specs = (
        P(None, None, "wide", "narrow"),
        P(None, None, "wide", "narrow"),
        P(None, "wide", "narrow"),
        P("wide", "narrow"),
        P("wide", "narrow"),
        P("wide", "narrow"),
        P("narrow", "wide", None),
        P("narrow", "wide"),
        P(None, "narrow", "wide"),
        P("narrow", "wide"),
    )
    out_specs = (P(None, None, "wide", "narrow"), P("wide", "narrow"), P())
    return jax.shard_map(
        on_device, mesh=mesh, in_specs=in_specs, out_specs=out_specs, check_vma=False
    )
```

```python
import jax
import jax.numpy as jnp
from jax import lax
from jax.experimental import pallas as pl
from jax.experimental.pallas import tpu as pltpu
from jax.sharding import PartitionSpec as P

ITERS = 2
KAPPA = 1024


def neighbour_sum(value):
    edges = []
    for axis, dim in (("wide", 2), ("narrow", 3)):
        peers, length = (lax.axis_size(axis), value.shape[dim])
        up = [(i, i + 1) for i in range(peers - 1)]
        down = [(j, i) for i, j in up]
        last = lax.slice_in_dim(value, length - 1, length, axis=dim)
        first = lax.slice_in_dim(value, 0, 1, axis=dim)
        before = lax.ppermute(last, axis, up)
        after = lax.ppermute(first, axis, down)
        inner_next = lax.slice_in_dim(value, 1, length, axis=dim)
        inner_prev = lax.slice_in_dim(value, 0, length - 1, axis=dim)
        edges.append(jnp.concatenate([inner_next, after], axis=dim))
        edges.append(jnp.concatenate([before, inner_prev], axis=dim))
    return edges[0] + edges[1] + edges[2] + edges[3]


def thomas(coupling, diagonal, right_side):
    layers = diagonal.shape[0]
    pivots = diagonal[0]
    ratios = [coupling[0] / pivots]
    partial_sol = [right_side[:, 0] / pivots]
    for level in range(1, layers):
        pivots = diagonal[level] - coupling[level - 1] * ratios[level - 1]
        if level < layers - 1:
            ratios.append(coupling[level] / pivots)
        partial_sol.append(
            (right_side[:, level] + coupling[level - 1] * partial_sol[level - 1]) / pivots
        )
    result = [partial_sol[layers - 1]]
    for level in range(layers - 2, -1, -1):
        result.append(partial_sol[level] + ratios[level] * result[-1])
    ordered = result[::-1]
    return jnp.stack(ordered, axis=1)


def make_diagonal(coupling, friction, horiz):
    zeros_row = jnp.zeros_like(coupling[:1])
    below = jnp.concatenate([zeros_row, coupling], axis=0)
    above = jnp.concatenate([coupling, zeros_row], axis=0)
    diagonal = 0.5 + 4.0 * horiz[None] + below + above
    return diagonal.at[0].add(friction)


def relax(beside_all, coupling, diagonal, horiz, ice_float, force):
    right_side = horiz * beside_all
    right_side = right_side.at[:, -1].add(force)
    return ice_float * thomas(coupling, diagonal, right_side)


def column_kernel(
    adjoint_ref,
    x_prev_ref,
    x_next_ref,
    y_prev_ref,
    y_next_ref,
    coupling_ref,
    friction_ref,
    horiz_ref,
    ice_ref,
    force_ref,
    out_ref,
    *rest,
):
    edge_refs, (ratio_ref, partial_ref) = rest[:-2], rest[-2:]
    comps, layers, rows_x, rows_y = adjoint_ref.shape
    rows = lax.broadcasted_iota(jnp.int32, (rows_x, rows_y), 0)
    cols = lax.broadcasted_iota(jnp.int32, (rows_x, rows_y), 1)
    horiz = horiz_ref[...]
    base = 0.5 + 4.0 * horiz

    def diagonal(level):
        value = base
        if level > 0:
            value = value + coupling_ref[level - 1]
        if level < layers - 1:
            value = value + coupling_ref[level]
        if level == 0:
            value = value + friction_ref[...]
        return value

    def beside(comp, level):
        center = adjoint_ref[comp, level]
        x_next = jnp.where(rows == rows_x - 1, x_next_ref[comp, level], pltpu.roll(center, rows_x - 1, 0))
        x_prev = jnp.where(rows == 0, x_prev_ref[comp, level], pltpu.roll(center, 1, 0))
        y_next = jnp.where(cols == rows_y - 1, y_next_ref[comp, level], pltpu.roll(center, rows_y - 1, 1))
        y_prev = jnp.where(cols == 0, y_prev_ref[comp, level], pltpu.roll(center, 1, 1))
        return x_next + x_prev + y_next + y_prev

    def right_side(comp, level):
        value = horiz * beside(comp, level)
        if level == layers - 1:
            value = value + force_ref[comp]
        return value

    pivots = diagonal(0)
    ratio_ref[0] = coupling_ref[0] / pivots
    for comp in range(comps):
        partial_ref[comp, 0] = right_side(comp, 0) / pivots
    for level in range(1, layers):
        below = coupling_ref[level - 1]
        pivots = diagonal(level) - below * ratio_ref[level - 1]
        if level < layers - 1:
            ratio_ref[level] = coupling_ref[level] / pivots
        for comp in range(comps):
            partial_ref[comp, level] = (
                right_side(comp, level) + below * partial_ref[comp, level - 1]
            ) / pivots
    ice = ice_ref[...]
    for comp in range(comps):
        result = partial_ref[comp, layers - 1]
        out_ref[comp, layers - 1] = ice * result
        for level in range(layers - 2, -1, -1):
            result = partial_ref[comp, level] + ratio_ref[level] * result
            out_ref[comp, level] = ice * result
    if edge_refs:
        last_row, first_row, last_col, first_col = edge_refs
        last_row[...] = out_ref[:, :, rows_x - 1 : rows_x, :]
        first_row[...] = out_ref[:, :, 0:1, :]
        for comp in range(comps):
            for level in range(layers):
                last_col[comp, level] = out_ref[comp, level, :, rows_y - 128 : rows_y][:, 127:128]
                first_col[comp, level] = out_ref[comp, level, :, 0:128][:, 0:1]


def block_edges(value):
    edges = []
    for dim in (2, 3):
        length = value.shape[dim]
        edges.append(lax.slice_in_dim(value, length - 1, length, axis=dim))
        edges.append(lax.slice_in_dim(value, 0, 1, axis=dim))
    return edges


def halo_edges(block):
    edges = []
    for index, axis in enumerate(("wide", "narrow")):
        peers = lax.axis_size(axis)
        up = [(i, i + 1) for i in range(peers - 1)]
        down = [(j, i) for i, j in up]
        for part, pairs in ((block[2 * index], up), (block[2 * index + 1], down)):
            if index:
                sent = lax.ppermute(part.reshape(part.shape[0], -1), axis, pairs)
                edges.append(sent.reshape(part.shape))
            else:
                edges.append(lax.ppermute(part, axis, pairs))
    return edges


def column_solve(adjoint, edges, coupling, friction, horiz, ice_float, force, with_edges):
    comps, layers, rows_x, rows_y = adjoint.shape
    cells = rows_x * rows_y
    out_shape = jax.ShapeDtypeStruct(adjoint.shape, jnp.float32)
    if with_edges:
        row = jax.ShapeDtypeStruct((comps, layers, 1, rows_y), jnp.float32)
        col = jax.ShapeDtypeStruct((comps, layers, rows_x, 1), jnp.float32)
        out_shape = (out_shape, row, row, col, col)
    return pl.pallas_call(
        column_kernel,
        out_shape=out_shape,
        scratch_shapes=[
            pltpu.VMEM((layers - 1, rows_x, rows_y), jnp.float32),
            pltpu.VMEM(adjoint.shape, jnp.float32),
        ],
        cost_estimate=pl.CostEstimate(
            flops=20 * comps * layers * cells,
            transcendentals=0,
            bytes_accessed=4 * cells * (2 * comps * layers + layers + 4),
        ),
    )(adjoint, *edges, coupling, friction, horiz, ice_float, force)


def cosine_table(length, after):
    block = 32
    freq = lax.broadcasted_iota(jnp.int32, (1, length), 1)
    freq, _ = lax.optimization_barrier((freq, after))
    coarse = lax.broadcasted_iota(jnp.int32, (length // block, 1), 0)
    fine = lax.broadcasted_iota(jnp.int32, (block, 1), 0)
    period = 4 * length
    scale = jnp.pi / (2.0 * length)
    coarse_angle = ((2 * block * coarse * freq) % period).astype(jnp.float32) * scale
    fine_angle = (((2 * fine + 1) * freq) % period).astype(jnp.float32) * scale
    table = (
        jnp.cos(coarse_angle)[:, None, :] * jnp.cos(fine_angle)[None, :, :]
        - jnp.sin(coarse_angle)[:, None, :] * jnp.sin(fine_angle)[None, :, :]
    ).reshape(length, length)
    norm_factor = jnp.where(freq == 0, jnp.sqrt(1.0 / length), jnp.sqrt(2.0 / length))
    return table * norm_factor.astype(jnp.float32)


def smooth_lines(lines, kappa_val, table):
    length = lines.shape[1]
    modes = lax.iota(jnp.int32, length).astype(jnp.float32)
    spectrum = 1.0 + kappa_val * (2.0 - 2.0 * jnp.cos(jnp.pi * modes / length))
    coefficients = jnp.dot(
        lines, table, precision=lax.Precision.HIGHEST, preferred_element_type=jnp.float32
    )
    coefficients = coefficients / spectrum[None, :]
    return lax.dot_general(
        coefficients,
        table,
        (((1,), (1,)), ((), ())),
        precision=lax.Precision.HIGHEST,
        preferred_element_type=jnp.float32,
    )


def split_parts(value):
    high = lax.reduce_precision(value, exponent_bits=8, mantissa_bits=7)
    rest = value - high
    middle = lax.reduce_precision(rest, exponent_bits=8, mantissa_bits=7)
    low = rest - middle
    return jnp.concatenate([high, middle, low], axis=0).astype(jnp.bfloat16)


def exact_dot(value, selector, contract):
    rows = value.shape[0]
    parts = lax.dot_general(
        split_parts(value),
        selector,
        (((1,), (contract,)), ((), ())),
        preferred_element_type=jnp.float32,
    )
    parts = parts.reshape(3, rows, parts.shape[-1])
    return (parts[0] + parts[1]) + parts[2]


def owner_ranks(owner_hot):
    count, peers = owner_hot.shape
    block = 128
    blocks = count // block
    hot = owner_hot.astype(jnp.bfloat16).reshape(blocks, block, peers)
    lower = (
        lax.broadcasted_iota(jnp.int32, (block, block), 0)
        >= lax.broadcasted_iota(jnp.int32, (block, block), 1)
    ).astype(jnp.bfloat16)
    within = jnp.einsum("ij,bjw->biw", lower, hot, preferred_element_type=jnp.float32)
    totals = within[:, -1, :].astype(jnp.bfloat16)
    strict = (
        lax.broadcasted_iota(jnp.int32, (blocks, blocks), 0)
        > lax.broadcasted_iota(jnp.int32, (blocks, blocks), 1)
    ).astype(jnp.bfloat16)
    before = jnp.dot(strict, totals, preferred_element_type=jnp.float32)
    counts = within + before[:, None, :]
    mine = jnp.where(owner_hot.reshape(blocks, block, peers), counts, 0.0)
    return jnp.sum(mine, axis=-1).reshape(count) - 1.0


def on_device(
    adjoint_start,
    velocity,
    coupling,
    friction,
    horiz,
    ice_mask,
    obs_owner,
    obs_cell,
    obs_value,
    obs_weight,
):
    wide_count = lax.axis_size("wide")
    rows_x, rows_y = friction.shape
    owners = obs_owner[0, :, 0]
    cell_ids = obs_cell[0]
    how_many = owners.shape[0]
    capacity = 2 * how_many // wide_count
    owner_hot = owners[:, None] == jnp.arange(wide_count, dtype=jnp.int32)[None, :]
    ranking = owner_ranks(owner_hot)
    rank_hot = (
        ranking[:, None] == jnp.arange(capacity, dtype=jnp.float32)[None, :]
    ).astype(jnp.bfloat16)
    payload = jnp.stack(
        [obs_value[0, 0], obs_value[1, 0], obs_weight[0], cell_ids.astype(jnp.float32)], axis=0
    )
    spread = jnp.where(owner_hot.T[None, :, :], payload[:, None, :], 0.0)
    packed = exact_dot(spread.reshape(4 * wide_count, how_many), rank_hot, 0)
    packed = packed.reshape(4, wide_count, capacity)
    arrived = lax.all_to_all(packed, "wide", split_axis=1, concat_axis=1, tiled=True).reshape(4, -1)
    target = arrived[3].astype(jnp.int32)
    slots = target.shape[0]
    column_hot = (
        jnp.arange(rows_y, dtype=jnp.int32)[:, None] == (target % rows_y)[None, :]
    ).astype(jnp.bfloat16)
    row_hot = jnp.arange(rows_x, dtype=jnp.int32)[:, None] == (target // rows_y)[None, :]
    top = velocity[:, -1].reshape(2 * rows_x, rows_y)
    picked = exact_dot(top, column_hot, 0).reshape(2, rows_x, slots)
    surface = jnp.sum(jnp.where(row_hot[None], picked, 0.0), axis=1)
    residual = surface - arrived[:2]
    weights = arrived[2]
    weighted = weights * residual
    placed = jnp.where(row_hot[None], weighted[:, None, :], 0.0).reshape(2 * rows_x, slots)
    force = exact_dot(placed, column_hot, 1).reshape(2, rows_x, rows_y)
    local_misfit = 0.5 * jnp.sum(weights * jnp.sum(residual * residual, axis=0))
    ice_float = ice_mask.astype(jnp.float32)
    adjoint = adjoint_start
    block = block_edges(adjoint)
    for sweep_no in range(ITERS):
        solved = column_solve(
            adjoint, halo_edges(block), coupling, friction, horiz, ice_float, force,
            sweep_no < ITERS - 1,
        )
        if sweep_no < ITERS - 1:
            adjoint, block = solved[0], list(solved[1:])
        else:
            adjoint = solved
    grad = -friction * ice_float * jnp.sum(adjoint[:, 0] * velocity[:, 0], axis=0)
    misfit_column = jnp.broadcast_to(local_misfit, (rows_y, 1))
    sent = jnp.concatenate([grad.T, misfit_column], axis=1)
    table = cosine_table(wide_count * rows_x, sent)
    lines = lax.all_to_all(sent, "wide", split_axis=0, concat_axis=1, tiled=True)
    width = lines.shape[0]
    lines = lines.reshape(width, wide_count, rows_x + 1)
    wide_misfit = jnp.sum(lines[0, :, rows_x])
    lines = lines[:, :, :rows_x].reshape(width, wide_count * rows_x)
    smooth = smooth_lines(lines, float(KAPPA), table)
    local_square = jnp.sum(smooth * smooth)
    square_column = jnp.broadcast_to(local_square, (width, wide_count, 1))
    returned = jnp.concatenate([smooth.reshape(width, wide_count, rows_x), square_column], axis=2)
    returned = returned.reshape(width, wide_count * (rows_x + 1))
    back = lax.all_to_all(returned, "wide", split_axis=1, concat_axis=0, tiled=True)
    wide_square = jnp.sum(back[::width, rows_x])
    back = back[:, :rows_x].T
    totals = lax.psum(jnp.stack([wide_square, wide_misfit]), "narrow")
    cell_total = wide_count * rows_x * rows_y * lax.axis_size("narrow")
    direction = back * lax.rsqrt(totals[0] / cell_total + 1e-06)
    return (adjoint, direction, totals[1])


def solution(mesh):
    in_specs = (
        P(None, None, "wide", "narrow"),
        P(None, None, "wide", "narrow"),
        P(None, "wide", "narrow"),
        P("wide", "narrow"),
        P("wide", "narrow"),
        P("wide", "narrow"),
        P("narrow", "wide", None),
        P("narrow", "wide"),
        P(None, "narrow", "wide"),
        P("narrow", "wide"),
    )
    out_specs = (P(None, None, "wide", "narrow"), P("wide", "narrow"), P())
    return jax.shard_map(
        on_device, mesh=mesh, in_specs=in_specs, out_specs=out_specs, check_vma=False
    )
```

```python
import jax
import jax.numpy as jnp
from jax import lax
from jax.experimental import pallas as pl
from jax.experimental.pallas import tpu as pltpu
from jax.sharding import PartitionSpec as P

ITERS = 2
KAPPA = 1024


def neighbour_sum(value):
    edges = []
    for axis, dim in (("wide", 2), ("narrow", 3)):
        peers, length = (lax.axis_size(axis), value.shape[dim])
        up = [(i, i + 1) for i in range(peers - 1)]
        down = [(j, i) for i, j in up]
        last = lax.slice_in_dim(value, length - 1, length, axis=dim)
        first = lax.slice_in_dim(value, 0, 1, axis=dim)
        before = lax.ppermute(last, axis, up)
        after = lax.ppermute(first, axis, down)
        inner_next = lax.slice_in_dim(value, 1, length, axis=dim)
        inner_prev = lax.slice_in_dim(value, 0, length - 1, axis=dim)
        edges.append(jnp.concatenate([inner_next, after], axis=dim))
        edges.append(jnp.concatenate([before, inner_prev], axis=dim))
    return edges[0] + edges[1] + edges[2] + edges[3]


def thomas(coupling, diagonal, right_side):
    layers = diagonal.shape[0]
    pivots = diagonal[0]
    ratios = [coupling[0] / pivots]
    partial_sol = [right_side[:, 0] / pivots]
    for level in range(1, layers):
        pivots = diagonal[level] - coupling[level - 1] * ratios[level - 1]
        if level < layers - 1:
            ratios.append(coupling[level] / pivots)
        partial_sol.append(
            (right_side[:, level] + coupling[level - 1] * partial_sol[level - 1]) / pivots
        )
    result = [partial_sol[layers - 1]]
    for level in range(layers - 2, -1, -1):
        result.append(partial_sol[level] + ratios[level] * result[-1])
    ordered = result[::-1]
    return jnp.stack(ordered, axis=1)


def make_diagonal(coupling, friction, horiz):
    zeros_row = jnp.zeros_like(coupling[:1])
    below = jnp.concatenate([zeros_row, coupling], axis=0)
    above = jnp.concatenate([coupling, zeros_row], axis=0)
    diagonal = 0.5 + 4.0 * horiz[None] + below + above
    return diagonal.at[0].add(friction)


def relax(beside_all, coupling, diagonal, horiz, ice_float, force):
    right_side = horiz * beside_all
    right_side = right_side.at[:, -1].add(force)
    return ice_float * thomas(coupling, diagonal, right_side)


def column_kernel(
    adjoint_ref,
    x_prev_ref,
    x_next_ref,
    y_prev_ref,
    y_next_ref,
    coupling_ref,
    friction_ref,
    horiz_ref,
    ice_ref,
    force_ref,
    out_ref,
    *rest,
):
    edge_refs, (ratio_ref, partial_ref) = rest[:-2], rest[-2:]
    comps, layers, rows_x, rows_y = adjoint_ref.shape
    rows = lax.broadcasted_iota(jnp.int32, (rows_x, rows_y), 0)
    cols = lax.broadcasted_iota(jnp.int32, (rows_x, rows_y), 1)
    horiz = horiz_ref[...]
    base = 0.5 + 4.0 * horiz

    def diagonal(level):
        value = base
        if level > 0:
            value = value + coupling_ref[level - 1]
        if level < layers - 1:
            value = value + coupling_ref[level]
        if level == 0:
            value = value + friction_ref[...]
        return value

    def beside(comp, level):
        center = adjoint_ref[comp, level]
        x_next = jnp.where(rows == rows_x - 1, x_next_ref[comp, level], pltpu.roll(center, rows_x - 1, 0))
        x_prev = jnp.where(rows == 0, x_prev_ref[comp, level], pltpu.roll(center, 1, 0))
        y_next = jnp.where(cols == rows_y - 1, y_next_ref[comp, level], pltpu.roll(center, rows_y - 1, 1))
        y_prev = jnp.where(cols == 0, y_prev_ref[comp, level], pltpu.roll(center, 1, 1))
        return x_next + x_prev + y_next + y_prev

    def right_side(comp, level):
        value = horiz * beside(comp, level)
        if level == layers - 1:
            value = value + force_ref[comp]
        return value

    pivots = diagonal(0)
    ratio_ref[0] = coupling_ref[0] / pivots
    for comp in range(comps):
        partial_ref[comp, 0] = right_side(comp, 0) / pivots
    for level in range(1, layers):
        below = coupling_ref[level - 1]
        pivots = diagonal(level) - below * ratio_ref[level - 1]
        if level < layers - 1:
            ratio_ref[level] = coupling_ref[level] / pivots
        for comp in range(comps):
            partial_ref[comp, level] = (
                right_side(comp, level) + below * partial_ref[comp, level - 1]
            ) / pivots
    ice = ice_ref[...]
    for comp in range(comps):
        result = partial_ref[comp, layers - 1]
        out_ref[comp, layers - 1] = ice * result
        for level in range(layers - 2, -1, -1):
            result = partial_ref[comp, level] + ratio_ref[level] * result
            out_ref[comp, level] = ice * result
    if edge_refs:
        last_row, first_row, last_col, first_col = edge_refs
        last_row[...] = out_ref[:, :, rows_x - 1 : rows_x, :]
        first_row[...] = out_ref[:, :, 0:1, :]
        for comp in range(comps):
            for level in range(layers):
                last_col[comp, level] = out_ref[comp, level, :, rows_y - 128 : rows_y][:, 127:128]
                first_col[comp, level] = out_ref[comp, level, :, 0:128][:, 0:1]


def block_edges(value):
    edges = []
    for dim in (2, 3):
        length = value.shape[dim]
        edges.append(lax.slice_in_dim(value, length - 1, length, axis=dim))
        edges.append(lax.slice_in_dim(value, 0, 1, axis=dim))
    return edges


def halo_edges(block):
    edges = []
    for index, axis in enumerate(("wide", "narrow")):
        peers = lax.axis_size(axis)
        up = [(i, i + 1) for i in range(peers - 1)]
        down = [(j, i) for i, j in up]
        edges.append(lax.ppermute(block[2 * index], axis, up))
        edges.append(lax.ppermute(block[2 * index + 1], axis, down))
    return edges


def column_solve(adjoint, edges, coupling, friction, horiz, ice_float, force, with_edges):
    comps, layers, rows_x, rows_y = adjoint.shape
    cells = rows_x * rows_y
    out_shape = jax.ShapeDtypeStruct(adjoint.shape, jnp.float32)
    if with_edges:
        row = jax.ShapeDtypeStruct((comps, layers, 1, rows_y), jnp.float32)
        col = jax.ShapeDtypeStruct((comps, layers, rows_x, 1), jnp.float32)
        out_shape = (out_shape, row, row, col, col)
    return pl.pallas_call(
        column_kernel,
        out_shape=out_shape,
        scratch_shapes=[
            pltpu.VMEM((layers - 1, rows_x, rows_y), jnp.float32),
            pltpu.VMEM(adjoint.shape, jnp.float32),
        ],
        cost_estimate=pl.CostEstimate(
            flops=20 * comps * layers * cells,
            transcendentals=0,
            bytes_accessed=4 * cells * (2 * comps * layers + layers + 4),
        ),
    )(adjoint, *edges, coupling, friction, horiz, ice_float, force)


def cosine_table(length, after):
    block = 32
    freq = lax.broadcasted_iota(jnp.int32, (1, length), 1)
    freq, _ = lax.optimization_barrier((freq, after))
    coarse = lax.broadcasted_iota(jnp.int32, (length // block, 1), 0)
    fine = lax.broadcasted_iota(jnp.int32, (block, 1), 0)
    period = 4 * length
    scale = jnp.pi / (2.0 * length)
    coarse_angle = ((2 * block * coarse * freq) % period).astype(jnp.float32) * scale
    fine_angle = (((2 * fine + 1) * freq) % period).astype(jnp.float32) * scale
    table = (
        jnp.cos(coarse_angle)[:, None, :] * jnp.cos(fine_angle)[None, :, :]
        - jnp.sin(coarse_angle)[:, None, :] * jnp.sin(fine_angle)[None, :, :]
    ).reshape(length, length)
    norm_factor = jnp.where(freq == 0, jnp.sqrt(1.0 / length), jnp.sqrt(2.0 / length))
    return table * norm_factor.astype(jnp.float32)


def smooth_lines(lines, kappa_val, table):
    length = lines.shape[1]
    modes = lax.iota(jnp.int32, length).astype(jnp.float32)
    spectrum = 1.0 + kappa_val * (2.0 - 2.0 * jnp.cos(jnp.pi * modes / length))
    coefficients = jnp.dot(
        lines, table, precision=lax.Precision.HIGHEST, preferred_element_type=jnp.float32
    )
    coefficients = coefficients / spectrum[None, :]
    return lax.dot_general(
        coefficients,
        table,
        (((1,), (1,)), ((), ())),
        precision=lax.Precision.HIGHEST,
        preferred_element_type=jnp.float32,
    )


def split_parts(value):
    high = lax.reduce_precision(value, exponent_bits=8, mantissa_bits=7)
    rest = value - high
    middle = lax.reduce_precision(rest, exponent_bits=8, mantissa_bits=7)
    low = rest - middle
    return jnp.concatenate([high, middle, low], axis=0).astype(jnp.bfloat16)


def exact_dot(value, selector, contract):
    rows = value.shape[0]
    parts = lax.dot_general(
        split_parts(value),
        selector,
        (((1,), (contract,)), ((), ())),
        preferred_element_type=jnp.float32,
    )
    parts = parts.reshape(3, rows, parts.shape[-1])
    return (parts[0] + parts[1]) + parts[2]


def owner_ranks(owner_hot):
    count, peers = owner_hot.shape
    block = 128
    blocks = count // block
    hot = owner_hot.astype(jnp.bfloat16).reshape(blocks, block, peers)
    lower = (
        lax.broadcasted_iota(jnp.int32, (block, block), 0)
        >= lax.broadcasted_iota(jnp.int32, (block, block), 1)
    ).astype(jnp.bfloat16)
    within = jnp.einsum("ij,bjw->biw", lower, hot, preferred_element_type=jnp.float32)
    totals = within[:, -1, :].astype(jnp.bfloat16)
    strict = (
        lax.broadcasted_iota(jnp.int32, (blocks, blocks), 0)
        > lax.broadcasted_iota(jnp.int32, (blocks, blocks), 1)
    ).astype(jnp.bfloat16)
    before = jnp.dot(strict, totals, preferred_element_type=jnp.float32)
    counts = within + before[:, None, :]
    mine = jnp.where(owner_hot.reshape(blocks, block, peers), counts, 0.0)
    return jnp.sum(mine, axis=-1).reshape(count) - 1.0


def on_device(
    adjoint_start,
    velocity,
    coupling,
    friction,
    horiz,
    ice_mask,
    obs_owner,
    obs_cell,
    obs_value,
    obs_weight,
):
    wide_count = lax.axis_size("wide")
    rows_x, rows_y = friction.shape
    owners = obs_owner[0, :, 0]
    cell_ids = obs_cell[0]
    how_many = owners.shape[0]
    capacity = 2 * how_many // wide_count
    owner_hot = owners[:, None] == jnp.arange(wide_count, dtype=jnp.int32)[None, :]
    ranking = owner_ranks(owner_hot)
    rank_hot = (
        ranking[:, None] == jnp.arange(capacity, dtype=jnp.float32)[None, :]
    ).astype(jnp.bfloat16)
    payload = jnp.stack(
        [obs_value[0, 0], obs_value[1, 0], obs_weight[0], cell_ids.astype(jnp.float32)], axis=0
    )
    spread = jnp.where(owner_hot.T[None, :, :], payload[:, None, :], 0.0)
    packed = exact_dot(spread.reshape(4 * wide_count, how_many), rank_hot, 0)
    packed = packed.reshape(4, wide_count, capacity)
    arrived = lax.all_to_all(packed, "wide", split_axis=1, concat_axis=1, tiled=True).reshape(4, -1)
    target = arrived[3].astype(jnp.int32)
    slots = target.shape[0]
    column_hot = (
        jnp.arange(rows_y, dtype=jnp.int32)[:, None] == (target % rows_y)[None, :]
    ).astype(jnp.bfloat16)
    row_hot = jnp.arange(rows_x, dtype=jnp.int32)[:, None] == (target // rows_y)[None, :]
    top = velocity[:, -1].reshape(2 * rows_x, rows_y)
    picked = exact_dot(top, column_hot, 0).reshape(2, rows_x, slots)
    surface = jnp.sum(jnp.where(row_hot[None], picked, 0.0), axis=1)
    residual = surface - arrived[:2]
    weights = arrived[2]
    weighted = weights * residual
    placed = jnp.where(row_hot[None], weighted[:, None, :], 0.0).reshape(2 * rows_x, slots)
    force = exact_dot(placed, column_hot, 1).reshape(2, rows_x, rows_y)
    local_misfit = 0.5 * jnp.sum(weights * jnp.sum(residual * residual, axis=0))
    ice_float = ice_mask.astype(jnp.float32)
    adjoint = adjoint_start
    block = block_edges(adjoint)
    for sweep_no in range(ITERS):
        solved = column_solve(
            adjoint, halo_edges(block), coupling, friction, horiz, ice_float, force,
            sweep_no < ITERS - 1,
        )
        if sweep_no < ITERS - 1:
            adjoint, block = solved[0], list(solved[1:])
        else:
            adjoint = solved
    grad = -friction * ice_float * jnp.sum(adjoint[:, 0] * velocity[:, 0], axis=0)
    misfit_column = jnp.broadcast_to(local_misfit, (rows_y, 1))
    sent = jnp.concatenate([grad.T, misfit_column], axis=1)
    table = cosine_table(wide_count * rows_x, sent)
    lines = lax.all_to_all(sent, "wide", split_axis=0, concat_axis=1, tiled=True)
    width = lines.shape[0]
    lines = lines.reshape(width, wide_count, rows_x + 1)
    wide_misfit = jnp.sum(lines[0, :, rows_x])
    lines = lines[:, :, :rows_x].reshape(width, wide_count * rows_x)
    smooth = smooth_lines(lines, float(KAPPA), table)
    local_square = jnp.sum(smooth * smooth)
    square_column = jnp.broadcast_to(local_square, (width, wide_count, 1))
    returned = jnp.concatenate([smooth.reshape(width, wide_count, rows_x), square_column], axis=2)
    returned = returned.reshape(width, wide_count * (rows_x + 1))
    back = lax.all_to_all(returned, "wide", split_axis=1, concat_axis=0, tiled=True)
    wide_square = jnp.sum(back[::width, rows_x])
    back = back[:, :rows_x].T
    back, wide_square = lax.optimization_barrier((back, wide_square))
    square_total, misfit_total = lax.psum((wide_square, wide_misfit), "narrow")
    cell_total = wide_count * rows_x * rows_y * lax.axis_size("narrow")
    direction = back * lax.rsqrt(square_total / cell_total + 1e-06)
    return (adjoint, direction, misfit_total)


def solution(mesh):
    in_specs = (
        P(None, None, "wide", "narrow"),
        P(None, None, "wide", "narrow"),
        P(None, "wide", "narrow"),
        P("wide", "narrow"),
        P("wide", "narrow"),
        P("wide", "narrow"),
        P("narrow", "wide", None),
        P("narrow", "wide"),
        P(None, "narrow", "wide"),
        P("narrow", "wide"),
    )
    out_specs = (P(None, None, "wide", "narrow"), P("wide", "narrow"), P())
    return jax.shard_map(
        on_device, mesh=mesh, in_specs=in_specs, out_specs=out_specs, check_vma=False
    )
```

```python
import jax
import jax.numpy as jnp
from jax import lax
from jax.experimental import pallas as pl
from jax.experimental.pallas import tpu as pltpu
from jax.sharding import PartitionSpec as P

ITERS = 2
KAPPA = 1024


def neighbour_sum(value):
    edges = []
    for axis, dim in (("wide", 2), ("narrow", 3)):
        peers, length = (lax.axis_size(axis), value.shape[dim])
        up = [(i, i + 1) for i in range(peers - 1)]
        down = [(j, i) for i, j in up]
        last = lax.slice_in_dim(value, length - 1, length, axis=dim)
        first = lax.slice_in_dim(value, 0, 1, axis=dim)
        before = lax.ppermute(last, axis, up)
        after = lax.ppermute(first, axis, down)
        inner_next = lax.slice_in_dim(value, 1, length, axis=dim)
        inner_prev = lax.slice_in_dim(value, 0, length - 1, axis=dim)
        edges.append(jnp.concatenate([inner_next, after], axis=dim))
        edges.append(jnp.concatenate([before, inner_prev], axis=dim))
    return edges[0] + edges[1] + edges[2] + edges[3]


def thomas(coupling, diagonal, right_side):
    layers = diagonal.shape[0]
    pivots = diagonal[0]
    ratios = [coupling[0] / pivots]
    partial_sol = [right_side[:, 0] / pivots]
    for level in range(1, layers):
        pivots = diagonal[level] - coupling[level - 1] * ratios[level - 1]
        if level < layers - 1:
            ratios.append(coupling[level] / pivots)
        partial_sol.append(
            (right_side[:, level] + coupling[level - 1] * partial_sol[level - 1]) / pivots
        )
    result = [partial_sol[layers - 1]]
    for level in range(layers - 2, -1, -1):
        result.append(partial_sol[level] + ratios[level] * result[-1])
    ordered = result[::-1]
    return jnp.stack(ordered, axis=1)


def make_diagonal(coupling, friction, horiz):
    zeros_row = jnp.zeros_like(coupling[:1])
    below = jnp.concatenate([zeros_row, coupling], axis=0)
    above = jnp.concatenate([coupling, zeros_row], axis=0)
    diagonal = 0.5 + 4.0 * horiz[None] + below + above
    return diagonal.at[0].add(friction)


def relax(beside_all, coupling, diagonal, horiz, ice_float, force):
    right_side = horiz * beside_all
    right_side = right_side.at[:, -1].add(force)
    return ice_float * thomas(coupling, diagonal, right_side)


def column_kernel(
    adjoint_ref,
    x_prev_ref,
    x_next_ref,
    y_prev_ref,
    y_next_ref,
    coupling_ref,
    friction_ref,
    horiz_ref,
    ice_ref,
    force_ref,
    out_ref,
    *rest,
):
    edge_refs, (ratio_ref, partial_ref) = rest[:-2], rest[-2:]
    comps, layers, rows_x, rows_y = adjoint_ref.shape
    rows = lax.broadcasted_iota(jnp.int32, (rows_x, rows_y), 0)
    cols = lax.broadcasted_iota(jnp.int32, (rows_x, rows_y), 1)
    horiz = horiz_ref[...]
    base = 0.5 + 4.0 * horiz

    def diagonal(level):
        value = base
        if level > 0:
            value = value + coupling_ref[level - 1]
        if level < layers - 1:
            value = value + coupling_ref[level]
        if level == 0:
            value = value + friction_ref[...]
        return value

    def beside(comp, level):
        center = adjoint_ref[comp, level]
        x_next = jnp.where(rows == rows_x - 1, x_next_ref[comp, level], pltpu.roll(center, rows_x - 1, 0))
        x_prev = jnp.where(rows == 0, x_prev_ref[comp, level], pltpu.roll(center, 1, 0))
        y_next = jnp.where(cols == rows_y - 1, y_next_ref[comp, level], pltpu.roll(center, rows_y - 1, 1))
        y_prev = jnp.where(cols == 0, y_prev_ref[comp, level], pltpu.roll(center, 1, 1))
        return x_next + x_prev + y_next + y_prev

    def right_side(comp, level):
        value = horiz * beside(comp, level)
        if level == layers - 1:
            value = value + force_ref[comp]
        return value

    pivots = diagonal(0)
    ratio_ref[0] = coupling_ref[0] / pivots
    for comp in range(comps):
        partial_ref[comp, 0] = right_side(comp, 0) / pivots
    for level in range(1, layers):
        below = coupling_ref[level - 1]
        pivots = diagonal(level) - below * ratio_ref[level - 1]
        if level < layers - 1:
            ratio_ref[level] = coupling_ref[level] / pivots
        for comp in range(comps):
            partial_ref[comp, level] = (
                right_side(comp, level) + below * partial_ref[comp, level - 1]
            ) / pivots
    ice = ice_ref[...]
    for comp in range(comps):
        result = partial_ref[comp, layers - 1]
        out_ref[comp, layers - 1] = ice * result
        for level in range(layers - 2, -1, -1):
            result = partial_ref[comp, level] + ratio_ref[level] * result
            out_ref[comp, level] = ice * result
    if edge_refs:
        last_row, first_row, last_col, first_col = edge_refs
        last_row[...] = out_ref[:, :, rows_x - 1 : rows_x, :]
        first_row[...] = out_ref[:, :, 0:1, :]
        for comp in range(comps):
            for level in range(layers):
                last_col[comp, level] = out_ref[comp, level, :, rows_y - 128 : rows_y][:, 127:128]
                first_col[comp, level] = out_ref[comp, level, :, 0:128][:, 0:1]


def block_edges(value):
    edges = []
    for dim in (2, 3):
        length = value.shape[dim]
        edges.append(lax.slice_in_dim(value, length - 1, length, axis=dim))
        edges.append(lax.slice_in_dim(value, 0, 1, axis=dim))
    return edges


def halo_edges(block):
    edges = []
    for index, axis in enumerate(("wide", "narrow")):
        peers = lax.axis_size(axis)
        up = [(i, i + 1) for i in range(peers - 1)]
        down = [(j, i) for i, j in up]
        edges.append(lax.ppermute(block[2 * index], axis, up))
        edges.append(lax.ppermute(block[2 * index + 1], axis, down))
    return edges


def column_solve(adjoint, edges, coupling, friction, horiz, ice_float, force, with_edges):
    comps, layers, rows_x, rows_y = adjoint.shape
    cells = rows_x * rows_y
    out_shape = jax.ShapeDtypeStruct(adjoint.shape, jnp.float32)
    if with_edges:
        row = jax.ShapeDtypeStruct((comps, layers, 1, rows_y), jnp.float32)
        col = jax.ShapeDtypeStruct((comps, layers, rows_x, 1), jnp.float32)
        out_shape = (out_shape, row, row, col, col)
    return pl.pallas_call(
        column_kernel,
        out_shape=out_shape,
        scratch_shapes=[
            pltpu.VMEM((layers - 1, rows_x, rows_y), jnp.float32),
            pltpu.VMEM(adjoint.shape, jnp.float32),
        ],
        cost_estimate=pl.CostEstimate(
            flops=20 * comps * layers * cells,
            transcendentals=0,
            bytes_accessed=4 * cells * (2 * comps * layers + layers + 4),
        ),
    )(adjoint, *edges, coupling, friction, horiz, ice_float, force)


def cosine_table(length, after):
    block = 32
    freq = lax.broadcasted_iota(jnp.int32, (1, length), 1)
    freq, _ = lax.optimization_barrier((freq, after))
    coarse = lax.broadcasted_iota(jnp.int32, (length // block, 1), 0)
    fine = lax.broadcasted_iota(jnp.int32, (block, 1), 0)
    period = 4 * length
    scale = jnp.pi / (2.0 * length)
    coarse_angle = ((2 * block * coarse * freq) % period).astype(jnp.float32) * scale
    fine_angle = (((2 * fine + 1) * freq) % period).astype(jnp.float32) * scale
    table = (
        jnp.cos(coarse_angle)[:, None, :] * jnp.cos(fine_angle)[None, :, :]
        - jnp.sin(coarse_angle)[:, None, :] * jnp.sin(fine_angle)[None, :, :]
    ).reshape(length, length)
    norm_factor = jnp.where(freq == 0, jnp.sqrt(1.0 / length), jnp.sqrt(2.0 / length))
    return table * norm_factor.astype(jnp.float32)


def smooth_lines(lines, kappa_val, table):
    length = lines.shape[1]
    modes = lax.iota(jnp.int32, length).astype(jnp.float32)
    spectrum = 1.0 + kappa_val * (2.0 - 2.0 * jnp.cos(jnp.pi * modes / length))
    coefficients = jnp.dot(
        lines, table, precision=lax.Precision.HIGH, preferred_element_type=jnp.float32
    )
    coefficients = coefficients / spectrum[None, :]
    return lax.dot_general(
        coefficients,
        table,
        (((1,), (1,)), ((), ())),
        precision=lax.Precision.HIGH,
        preferred_element_type=jnp.float32,
    )


def split_parts(value):
    high = lax.reduce_precision(value, exponent_bits=8, mantissa_bits=7)
    rest = value - high
    middle = lax.reduce_precision(rest, exponent_bits=8, mantissa_bits=7)
    low = rest - middle
    return jnp.concatenate([high, middle, low], axis=0).astype(jnp.bfloat16)


def exact_dot(value, selector, contract):
    rows = value.shape[0]
    parts = lax.dot_general(
        split_parts(value),
        selector,
        (((1,), (contract,)), ((), ())),
        preferred_element_type=jnp.float32,
    )
    parts = parts.reshape(3, rows, parts.shape[-1])
    return (parts[0] + parts[1]) + parts[2]


def owner_ranks(owner_hot):
    count, peers = owner_hot.shape
    block = 128
    blocks = count // block
    hot = owner_hot.astype(jnp.bfloat16).reshape(blocks, block, peers)
    lower = (
        lax.broadcasted_iota(jnp.int32, (block, block), 0)
        >= lax.broadcasted_iota(jnp.int32, (block, block), 1)
    ).astype(jnp.bfloat16)
    within = jnp.einsum("ij,bjw->biw", lower, hot, preferred_element_type=jnp.float32)
    totals = within[:, -1, :].astype(jnp.bfloat16)
    strict = (
        lax.broadcasted_iota(jnp.int32, (blocks, blocks), 0)
        > lax.broadcasted_iota(jnp.int32, (blocks, blocks), 1)
    ).astype(jnp.bfloat16)
    before = jnp.dot(strict, totals, preferred_element_type=jnp.float32)
    counts = within + before[:, None, :]
    mine = jnp.where(owner_hot.reshape(blocks, block, peers), counts, 0.0)
    return jnp.sum(mine, axis=-1).reshape(count) - 1.0


def on_device(
    adjoint_start,
    velocity,
    coupling,
    friction,
    horiz,
    ice_mask,
    obs_owner,
    obs_cell,
    obs_value,
    obs_weight,
):
    wide_count = lax.axis_size("wide")
    rows_x, rows_y = friction.shape
    owners = obs_owner[0, :, 0]
    cell_ids = obs_cell[0]
    how_many = owners.shape[0]
    capacity = 2 * how_many // wide_count
    owner_hot = owners[:, None] == jnp.arange(wide_count, dtype=jnp.int32)[None, :]
    ranking = owner_ranks(owner_hot)
    rank_hot = (
        ranking[:, None] == jnp.arange(capacity, dtype=jnp.float32)[None, :]
    ).astype(jnp.bfloat16)
    payload = jnp.stack(
        [obs_value[0, 0], obs_value[1, 0], obs_weight[0], cell_ids.astype(jnp.float32)], axis=0
    )
    spread = jnp.where(owner_hot.T[None, :, :], payload[:, None, :], 0.0)
    packed = exact_dot(spread.reshape(4 * wide_count, how_many), rank_hot, 0)
    packed = packed.reshape(4, wide_count, capacity)
    arrived = lax.all_to_all(packed, "wide", split_axis=1, concat_axis=1, tiled=True).reshape(4, -1)
    target = arrived[3].astype(jnp.int32)
    slots = target.shape[0]
    column_hot = (
        jnp.arange(rows_y, dtype=jnp.int32)[:, None] == (target % rows_y)[None, :]
    ).astype(jnp.bfloat16)
    row_hot = jnp.arange(rows_x, dtype=jnp.int32)[:, None] == (target // rows_y)[None, :]
    top = velocity[:, -1].reshape(2 * rows_x, rows_y)
    picked = exact_dot(top, column_hot, 0).reshape(2, rows_x, slots)
    surface = jnp.sum(jnp.where(row_hot[None], picked, 0.0), axis=1)
    residual = surface - arrived[:2]
    weights = arrived[2]
    weighted = weights * residual
    placed = jnp.where(row_hot[None], weighted[:, None, :], 0.0).reshape(2 * rows_x, slots)
    force = exact_dot(placed, column_hot, 1).reshape(2, rows_x, rows_y)
    local_misfit = 0.5 * jnp.sum(weights * jnp.sum(residual * residual, axis=0))
    ice_float = ice_mask.astype(jnp.float32)
    adjoint = adjoint_start
    block = block_edges(adjoint)
    for sweep_no in range(ITERS):
        solved = column_solve(
            adjoint, halo_edges(block), coupling, friction, horiz, ice_float, force,
            sweep_no < ITERS - 1,
        )
        if sweep_no < ITERS - 1:
            adjoint, block = solved[0], list(solved[1:])
        else:
            adjoint = solved
    grad = -friction * ice_float * jnp.sum(adjoint[:, 0] * velocity[:, 0], axis=0)
    misfit_column = jnp.broadcast_to(local_misfit, (rows_y, 1))
    sent = jnp.concatenate([grad.T, misfit_column], axis=1)
    table = cosine_table(wide_count * rows_x, sent)
    lines = lax.all_to_all(sent, "wide", split_axis=0, concat_axis=1, tiled=True)
    width = lines.shape[0]
    lines = lines.reshape(width, wide_count, rows_x + 1)
    wide_misfit = jnp.sum(lines[0, :, rows_x])
    lines = lines[:, :, :rows_x].reshape(width, wide_count * rows_x)
    smooth = smooth_lines(lines, float(KAPPA), table)
    local_square = jnp.sum(smooth * smooth)
    square_column = jnp.broadcast_to(local_square, (width, wide_count, 1))
    returned = jnp.concatenate([smooth.reshape(width, wide_count, rows_x), square_column], axis=2)
    returned = returned.reshape(width, wide_count * (rows_x + 1))
    back = lax.all_to_all(returned, "wide", split_axis=1, concat_axis=0, tiled=True)
    wide_square = jnp.sum(back[::width, rows_x])
    back = back[:, :rows_x].T
    back, wide_square = lax.optimization_barrier((back, wide_square))
    square_total, misfit_total = lax.psum((wide_square, wide_misfit), "narrow")
    cell_total = wide_count * rows_x * rows_y * lax.axis_size("narrow")
    direction = back * lax.rsqrt(square_total / cell_total + 1e-06)
    return (adjoint, direction, misfit_total)


def solution(mesh):
    in_specs = (
        P(None, None, "wide", "narrow"),
        P(None, None, "wide", "narrow"),
        P(None, "wide", "narrow"),
        P("wide", "narrow"),
        P("wide", "narrow"),
        P("wide", "narrow"),
        P("narrow", "wide", None),
        P("narrow", "wide"),
        P(None, "narrow", "wide"),
        P("narrow", "wide"),
    )
    out_specs = (P(None, None, "wide", "narrow"), P("wide", "narrow"), P())
    return jax.shard_map(
        on_device, mesh=mesh, in_specs=in_specs, out_specs=out_specs, check_vma=False
    )
```

```python
import jax
import jax.numpy as jnp
from jax import lax
from jax.experimental import pallas as pl
from jax.experimental.pallas import tpu as pltpu
from jax.sharding import PartitionSpec as P

ITERS = 2
KAPPA = 1024


def neighbour_sum(value):
    edges = []
    for axis, dim in (("wide", 2), ("narrow", 3)):
        peers, length = (lax.axis_size(axis), value.shape[dim])
        up = [(i, i + 1) for i in range(peers - 1)]
        down = [(j, i) for i, j in up]
        last = lax.slice_in_dim(value, length - 1, length, axis=dim)
        first = lax.slice_in_dim(value, 0, 1, axis=dim)
        before = lax.ppermute(last, axis, up)
        after = lax.ppermute(first, axis, down)
        inner_next = lax.slice_in_dim(value, 1, length, axis=dim)
        inner_prev = lax.slice_in_dim(value, 0, length - 1, axis=dim)
        edges.append(jnp.concatenate([inner_next, after], axis=dim))
        edges.append(jnp.concatenate([before, inner_prev], axis=dim))
    return edges[0] + edges[1] + edges[2] + edges[3]


def thomas(coupling, diagonal, right_side):
    layers = diagonal.shape[0]
    pivots = diagonal[0]
    ratios = [coupling[0] / pivots]
    partial_sol = [right_side[:, 0] / pivots]
    for level in range(1, layers):
        pivots = diagonal[level] - coupling[level - 1] * ratios[level - 1]
        if level < layers - 1:
            ratios.append(coupling[level] / pivots)
        partial_sol.append(
            (right_side[:, level] + coupling[level - 1] * partial_sol[level - 1]) / pivots
        )
    result = [partial_sol[layers - 1]]
    for level in range(layers - 2, -1, -1):
        result.append(partial_sol[level] + ratios[level] * result[-1])
    ordered = result[::-1]
    return jnp.stack(ordered, axis=1)


def make_diagonal(coupling, friction, horiz):
    zeros_row = jnp.zeros_like(coupling[:1])
    below = jnp.concatenate([zeros_row, coupling], axis=0)
    above = jnp.concatenate([coupling, zeros_row], axis=0)
    diagonal = 0.5 + 4.0 * horiz[None] + below + above
    return diagonal.at[0].add(friction)


def relax(beside_all, coupling, diagonal, horiz, ice_float, force):
    right_side = horiz * beside_all
    right_side = right_side.at[:, -1].add(force)
    return ice_float * thomas(coupling, diagonal, right_side)


def column_kernel(
    adjoint_ref,
    x_prev_ref,
    x_next_ref,
    y_prev_ref,
    y_next_ref,
    coupling_ref,
    friction_ref,
    horiz_ref,
    ice_ref,
    force_ref,
    out_ref,
    *rest,
):
    edge_refs, (ratio_ref, partial_ref) = rest[:-2], rest[-2:]
    comps, layers, rows_x, rows_y = adjoint_ref.shape
    rows = lax.broadcasted_iota(jnp.int32, (rows_x, rows_y), 0)
    cols = lax.broadcasted_iota(jnp.int32, (rows_x, rows_y), 1)
    horiz = horiz_ref[...]
    base = 0.5 + 4.0 * horiz

    def diagonal(level):
        value = base
        if level > 0:
            value = value + coupling_ref[level - 1]
        if level < layers - 1:
            value = value + coupling_ref[level]
        if level == 0:
            value = value + friction_ref[...]
        return value

    def beside(comp, level):
        center = adjoint_ref[comp, level]
        x_next = jnp.where(rows == rows_x - 1, x_next_ref[comp, level], pltpu.roll(center, rows_x - 1, 0))
        x_prev = jnp.where(rows == 0, x_prev_ref[comp, level], pltpu.roll(center, 1, 0))
        y_next = jnp.where(cols == rows_y - 1, y_next_ref[comp, level], pltpu.roll(center, rows_y - 1, 1))
        y_prev = jnp.where(cols == 0, y_prev_ref[comp, level], pltpu.roll(center, 1, 1))
        return x_next + x_prev + y_next + y_prev

    def right_side(comp, level):
        value = horiz * beside(comp, level)
        if level == layers - 1:
            value = value + force_ref[comp]
        return value

    pivots = diagonal(0)
    ratio_ref[0] = coupling_ref[0] / pivots
    for comp in range(comps):
        partial_ref[comp, 0] = right_side(comp, 0) / pivots
    for level in range(1, layers):
        below = coupling_ref[level - 1]
        pivots = diagonal(level) - below * ratio_ref[level - 1]
        if level < layers - 1:
            ratio_ref[level] = coupling_ref[level] / pivots
        for comp in range(comps):
            partial_ref[comp, level] = (
                right_side(comp, level) + below * partial_ref[comp, level - 1]
            ) / pivots
    ice = ice_ref[...]
    for comp in range(comps):
        result = partial_ref[comp, layers - 1]
        out_ref[comp, layers - 1] = ice * result
        for level in range(layers - 2, -1, -1):
            result = partial_ref[comp, level] + ratio_ref[level] * result
            out_ref[comp, level] = ice * result
    if edge_refs:
        last_row, first_row, last_col, first_col = edge_refs
        last_row[...] = out_ref[:, :, rows_x - 1 : rows_x, :]
        first_row[...] = out_ref[:, :, 0:1, :]
        for comp in range(comps):
            for level in range(layers):
                last_col[comp, level] = out_ref[comp, level, :, rows_y - 128 : rows_y][:, 127:128]
                first_col[comp, level] = out_ref[comp, level, :, 0:128][:, 0:1]


def block_edges(value):
    edges = []
    for dim in (2, 3):
        length = value.shape[dim]
        edges.append(lax.slice_in_dim(value, length - 1, length, axis=dim))
        edges.append(lax.slice_in_dim(value, 0, 1, axis=dim))
    return edges


def halo_edges(block):
    edges = []
    for index, axis in enumerate(("wide", "narrow")):
        peers = lax.axis_size(axis)
        up = [(i, i + 1) for i in range(peers - 1)]
        down = [(j, i) for i, j in up]
        edges.append(lax.ppermute(block[2 * index], axis, up))
        edges.append(lax.ppermute(block[2 * index + 1], axis, down))
    return edges


def column_solve(adjoint, edges, coupling, friction, horiz, ice_float, force, with_edges):
    comps, layers, rows_x, rows_y = adjoint.shape
    cells = rows_x * rows_y
    out_shape = jax.ShapeDtypeStruct(adjoint.shape, jnp.float32)
    if with_edges:
        row = jax.ShapeDtypeStruct((comps, layers, 1, rows_y), jnp.float32)
        col = jax.ShapeDtypeStruct((comps, layers, rows_x, 1), jnp.float32)
        out_shape = (out_shape, row, row, col, col)
    return pl.pallas_call(
        column_kernel,
        out_shape=out_shape,
        scratch_shapes=[
            pltpu.VMEM((layers - 1, rows_x, rows_y), jnp.float32),
            pltpu.VMEM(adjoint.shape, jnp.float32),
        ],
        cost_estimate=pl.CostEstimate(
            flops=20 * comps * layers * cells,
            transcendentals=0,
            bytes_accessed=4 * cells * (2 * comps * layers + layers + 4),
        ),
    )(adjoint, *edges, coupling, friction, horiz, ice_float, force)


def cosine_table(length, after):
    block = 32
    freq = lax.broadcasted_iota(jnp.int32, (1, length), 1)
    freq, _ = lax.optimization_barrier((freq, after))
    coarse = lax.broadcasted_iota(jnp.int32, (length // block, 1), 0)
    fine = lax.broadcasted_iota(jnp.int32, (block, 1), 0)
    period = 4 * length
    scale = jnp.pi / (2.0 * length)
    coarse_angle = ((2 * block * coarse * freq) % period).astype(jnp.float32) * scale
    fine_angle = (((2 * fine + 1) * freq) % period).astype(jnp.float32) * scale
    table = (
        jnp.cos(coarse_angle)[:, None, :] * jnp.cos(fine_angle)[None, :, :]
        - jnp.sin(coarse_angle)[:, None, :] * jnp.sin(fine_angle)[None, :, :]
    ).reshape(length, length)
    norm_factor = jnp.where(freq == 0, jnp.sqrt(1.0 / length), jnp.sqrt(2.0 / length))
    return table * norm_factor.astype(jnp.float32)


def smooth_lines(lines, kappa_val, table):
    length = lines.shape[1]
    modes = lax.iota(jnp.int32, length).astype(jnp.float32)
    spectrum = 1.0 + kappa_val * (2.0 - 2.0 * jnp.cos(jnp.pi * modes / length))
    coefficients = jnp.dot(
        lines, table, precision=lax.Precision.HIGH, preferred_element_type=jnp.float32
    )
    coefficients = coefficients / spectrum[None, :]
    return lax.dot_general(
        coefficients,
        table,
        (((1,), (1,)), ((), ())),
        precision=lax.Precision.HIGH,
        preferred_element_type=jnp.float32,
    )


def split_parts(value):
    high = lax.reduce_precision(value, exponent_bits=8, mantissa_bits=7)
    rest = value - high
    return jnp.concatenate([high, rest], axis=0).astype(jnp.bfloat16)


def exact_dot(value, selector, contract):
    rows = value.shape[0]
    parts = lax.dot_general(
        split_parts(value),
        selector,
        (((1,), (contract,)), ((), ())),
        preferred_element_type=jnp.float32,
    )
    parts = parts.reshape(2, rows, parts.shape[-1])
    return parts[0] + parts[1]


def owner_ranks(owner_hot):
    count, peers = owner_hot.shape
    block = 128
    blocks = count // block
    hot = owner_hot.astype(jnp.bfloat16).reshape(blocks, block, peers)
    lower = (
        lax.broadcasted_iota(jnp.int32, (block, block), 0)
        >= lax.broadcasted_iota(jnp.int32, (block, block), 1)
    ).astype(jnp.bfloat16)
    within = jnp.einsum("ij,bjw->biw", lower, hot, preferred_element_type=jnp.float32)
    totals = within[:, -1, :].astype(jnp.bfloat16)
    strict = (
        lax.broadcasted_iota(jnp.int32, (blocks, blocks), 0)
        > lax.broadcasted_iota(jnp.int32, (blocks, blocks), 1)
    ).astype(jnp.bfloat16)
    before = jnp.dot(strict, totals, preferred_element_type=jnp.float32)
    counts = within + before[:, None, :]
    mine = jnp.where(owner_hot.reshape(blocks, block, peers), counts, 0.0)
    return jnp.sum(mine, axis=-1).reshape(count) - 1.0


def on_device(
    adjoint_start,
    velocity,
    coupling,
    friction,
    horiz,
    ice_mask,
    obs_owner,
    obs_cell,
    obs_value,
    obs_weight,
):
    wide_count = lax.axis_size("wide")
    rows_x, rows_y = friction.shape
    owners = obs_owner[0, :, 0]
    cell_ids = obs_cell[0]
    how_many = owners.shape[0]
    capacity = 2 * how_many // wide_count
    owner_hot = owners[:, None] == jnp.arange(wide_count, dtype=jnp.int32)[None, :]
    ranking = owner_ranks(owner_hot)
    rank_hot = (
        ranking[:, None] == jnp.arange(capacity, dtype=jnp.float32)[None, :]
    ).astype(jnp.bfloat16)
    payload = jnp.stack(
        [obs_value[0, 0], obs_value[1, 0], obs_weight[0], cell_ids.astype(jnp.float32)], axis=0
    )
    spread = jnp.where(owner_hot.T[None, :, :], payload[:, None, :], 0.0)
    packed = exact_dot(spread.reshape(4 * wide_count, how_many), rank_hot, 0)
    packed = packed.reshape(4, wide_count, capacity)
    arrived = lax.all_to_all(packed, "wide", split_axis=1, concat_axis=1, tiled=True).reshape(4, -1)
    target = arrived[3].astype(jnp.int32)
    slots = target.shape[0]
    column_hot = (
        jnp.arange(rows_y, dtype=jnp.int32)[:, None] == (target % rows_y)[None, :]
    ).astype(jnp.bfloat16)
    row_hot = jnp.arange(rows_x, dtype=jnp.int32)[:, None] == (target // rows_y)[None, :]
    top = velocity[:, -1].reshape(2 * rows_x, rows_y)
    picked = exact_dot(top, column_hot, 0).reshape(2, rows_x, slots)
    surface = jnp.sum(jnp.where(row_hot[None], picked, 0.0), axis=1)
    residual = surface - arrived[:2]
    weights = arrived[2]
    weighted = weights * residual
    placed = jnp.where(row_hot[None], weighted[:, None, :], 0.0).reshape(2 * rows_x, slots)
    force = exact_dot(placed, column_hot, 1).reshape(2, rows_x, rows_y)
    local_misfit = 0.5 * jnp.sum(weights * jnp.sum(residual * residual, axis=0))
    ice_float = ice_mask.astype(jnp.float32)
    adjoint = adjoint_start
    block = block_edges(adjoint)
    for sweep_no in range(ITERS):
        solved = column_solve(
            adjoint, halo_edges(block), coupling, friction, horiz, ice_float, force,
            sweep_no < ITERS - 1,
        )
        if sweep_no < ITERS - 1:
            adjoint, block = solved[0], list(solved[1:])
        else:
            adjoint = solved
    grad = -friction * ice_float * jnp.sum(adjoint[:, 0] * velocity[:, 0], axis=0)
    misfit_column = jnp.broadcast_to(local_misfit, (rows_y, 1))
    sent = jnp.concatenate([grad.T, misfit_column], axis=1)
    table = cosine_table(wide_count * rows_x, sent)
    lines = lax.all_to_all(sent, "wide", split_axis=0, concat_axis=1, tiled=True)
    width = lines.shape[0]
    lines = lines.reshape(width, wide_count, rows_x + 1)
    wide_misfit = jnp.sum(lines[0, :, rows_x])
    lines = lines[:, :, :rows_x].reshape(width, wide_count * rows_x)
    smooth = smooth_lines(lines, float(KAPPA), table)
    local_square = jnp.sum(smooth * smooth)
    square_column = jnp.broadcast_to(local_square, (width, wide_count, 1))
    returned = jnp.concatenate([smooth.reshape(width, wide_count, rows_x), square_column], axis=2)
    returned = returned.reshape(width, wide_count * (rows_x + 1))
    back = lax.all_to_all(returned, "wide", split_axis=1, concat_axis=0, tiled=True)
    wide_square = jnp.sum(back[::width, rows_x])
    back = back[:, :rows_x].T
    back, wide_square = lax.optimization_barrier((back, wide_square))
    square_total, misfit_total = lax.psum((wide_square, wide_misfit), "narrow")
    cell_total = wide_count * rows_x * rows_y * lax.axis_size("narrow")
    direction = back * lax.rsqrt(square_total / cell_total + 1e-06)
    return (adjoint, direction, misfit_total)


def solution(mesh):
    in_specs = (
        P(None, None, "wide", "narrow"),
        P(None, None, "wide", "narrow"),
        P(None, "wide", "narrow"),
        P("wide", "narrow"),
        P("wide", "narrow"),
        P("wide", "narrow"),
        P("narrow", "wide", None),
        P("narrow", "wide"),
        P(None, "narrow", "wide"),
        P("narrow", "wide"),
    )
    out_specs = (P(None, None, "wide", "narrow"), P("wide", "narrow"), P())
    return jax.shard_map(
        on_device, mesh=mesh, in_specs=in_specs, out_specs=out_specs, check_vma=False
    )
```
